256 devices in a mesh: scene: 4 (over x), region: 64 (over z, y, core).
Axes of the slice: x: 4, y: 4, z: 8, core: 2. Of those that a mesh axis runs over, the one named last changes fastest.
Arguments:
- features: bfloat16 [4, 64, 1728, 128], P('scene', 'region'), may hold values from -6 to 6
- voxel_mask: int32 [4, 64, 1728], P('scene', 'region'), may hold values 0 or 1
- cotangent: bfloat16 [4, 64, 1728, 128], P('scene', 'region'), may hold values from -6 to 6
- norm_gain: float32 [128], replicated, may hold values from 0.1 to 1.9
- conv_weight: bfloat16 [27, 128, 128], replicated, may hold values from -0.109375 to 0.109375
- block_owner: int32 [4, 64], P('scene'), may hold values from 0 to 63, each once within a row
Outputs:
- block_output: bfloat16 [4, 64, 1728, 128], P('scene', 'region')
- input_grad: bfloat16 [4, 64, 1728, 128], P('scene', 'region')
- weight_update: float32 [3456, 128], P('region')
The draws below stay inside these ranges and needn't reach their ends.
Inputs may be any that keep to these rules, and one draw needn't show every extreme that they name: `block_owner`: each row names every slot of the scene exactly once.
All inputs are finite; a program needn't handle non-finite values. No bound on the sum of `voxel_mask` on one device may be relied on, other than what follows from the above.
Results may differ from the reference program's by a relative error of at most 0.0029.
Values may be sent and summed in bfloat16 or wider, within the bound.
No kernel may reach another device: no remote copies, remote signals or barrier semaphores. Data moves between devices by JAX's collectives and lax.ppermute only.
A program may use at most 128 MiB of HBM per device.

```python
import math
import jax
import jax.numpy as jnp
from jax import lax

C = 128
BS = 12
TAPS = 27
GY = 4
GZ = 2
GX = 8
SLOTS = 64
SCENES = 4
VOX = 1728


def place_ends(result, stream_key, low, high):
    longest = result.shape.index(max(result.shape))
    spots = []
    for shift in (0, 1):
        where = [jax.random.randint(jax.random.fold_in(stream_key, axis), (), 0, length) for axis, length in enumerate(result.shape)]
        where[longest] = (where[longest] + shift) % result.shape[longest]
        spots.append(tuple(where))
    return result.at[spots[0]].set(low).at[spots[1]].set(high)


def block_scale(stream_key, dims, shards, smallest, high):
    gain = 1.0
    for dim, blocks in shards:
        steps = jax.random.uniform(jax.random.fold_in(jax.random.fold_in(stream_key, 6), dim), (blocks,), jnp.float32, smallest / len(shards), high / len(shards))
        gain = gain * jnp.repeat(jnp.exp(steps), dims[dim] // blocks).reshape((-1,) + (1,) * (len(dims) - 1 - dim))
    return gain


def centred(own_key, extent, scale, most, pieces=(), kind=jnp.bfloat16):
    entries = scale * jax.random.normal(own_key, extent, jnp.float32)
    if pieces:
        entries = entries * block_scale(own_key, extent, pieces, -0.22, 0.18)
    return jnp.clip(entries, -most, most).astype(kind)


def setup_inputs(seed: int = 0) -> dict:
    key_list = jax.random.split(jax.random.key(seed), 7)
    return {
        "features": centred(key_list[0], (SCENES, SLOTS, VOX, C), 1.0, 6.0, ((0, 4), (1, 64))),
        "voxel_mask": place_ends((jax.random.randint(key_list[1], (SCENES, SLOTS, VOX), 0, 2) < 1).astype(jnp.int32), jax.random.fold_in(key_list[1], 1), 0, 1),
        "cotangent": centred(key_list[2], (SCENES, SLOTS, VOX, C), 1.0, 6.0, ((0, 4), (1, 64))),
        "norm_gain": jnp.clip(1.0 + 0.18 * jax.random.normal(key_list[3], (C,), jnp.float32), 0.1, 1.9),
        "conv_weight": centred(key_list[4], (TAPS, C, C), (TAPS * C) ** -0.5, 0.109375),
        "block_owner": jax.vmap(lambda own: jax.random.permutation(own, SLOTS))(jax.random.split(key_list[5], SCENES)).reshape((SCENES, SLOTS)).astype(jnp.int32),
    }


NORM_EPSILON = 1e-06
OFFSETS = [(a, b, c) for a in (-1, 0, 1) for b in (-1, 0, 1) for c in (-1, 0, 1)]

def to_grid(blocks):
    width = blocks.shape[-1]
    cube = blocks.reshape(GX, GY, GZ, BS, BS, BS, width)
    cube = cube.transpose(0, 3, 1, 4, 2, 5, 6).reshape(GX * BS, GY * BS, GZ * BS, width)
    return jnp.pad(cube, ((1, 1), (1, 1), (1, 1), (0, 0)))

def scene_pass(x_blocks, mask_blocks, cot_blocks, norm_gain, conv_weight):
    inputs = x_blocks.astype(jnp.float32)
    mask_col = mask_blocks.astype(jnp.float32)[..., None]
    rinv = lax.rsqrt(lax.optimization_barrier(jnp.mean(inputs * inputs, axis=-1, keepdims=True)) + NORM_EPSILON)
    normed = inputs * rinv
    pre = normed * norm_gain
    activity = (jax.nn.silu(pre) * mask_col).astype(jnp.bfloat16)
    grad_out = cot_blocks * mask_blocks.astype(jnp.bfloat16)[..., None]
    act_grid = to_grid(activity)
    grad_grid = to_grid(grad_out)
    width = x_blocks.shape[-1]

    def step(weight_grad, block_index):
        block_x = block_index // (GY * GZ)
        block_y = block_index // GZ % GY
        block_z = block_index % GZ
        zero_index = jnp.zeros((), jnp.int32)
        starts = (block_x * BS, block_y * BS, block_z * BS, zero_index)
        window_act = lax.dynamic_slice(act_grid, starts, (BS + 2, BS + 2, BS + 2, width))
        window_grad = lax.dynamic_slice(grad_grid, starts, (BS + 2, BS + 2, BS + 2, width))
        grad_block = lax.dynamic_index_in_dim(grad_out, block_index, 0, keepdims=False)
        forward = jnp.zeros((BS * BS * BS, width), jnp.float32)
        backward = jnp.zeros((BS * BS * BS, width), jnp.float32)
        terms = []
        for tap_index, (shift_x, shift_y, shift_z) in enumerate(OFFSETS):
            window = window_act[1 + shift_x:1 + shift_x + BS, 1 + shift_y:1 + shift_y + BS, 1 + shift_z:1 + shift_z + BS].reshape(-1, width)
            forward = forward + jnp.dot(window, conv_weight[tap_index], preferred_element_type=jnp.float32)
            mirror = window_grad[1 - shift_x:1 - shift_x + BS, 1 - shift_y:1 - shift_y + BS, 1 - shift_z:1 - shift_z + BS].reshape(-1, width)
            backward = backward + lax.dot_general(mirror, conv_weight[tap_index], (((1,), (1,)), ((), ())), preferred_element_type=jnp.float32)
            terms.append(lax.dot_general(window, grad_block, (((0,), (0,)), ((), ())), preferred_element_type=jnp.float32))
        return (weight_grad + jnp.stack(terms), (forward, backward))
    start_grad = jnp.zeros((TAPS, width, width), jnp.float32)
    weight_grad, (forward, backward) = lax.scan(step, start_grad, jnp.arange(SLOTS, dtype=jnp.int32))
    block_output = (inputs + forward * mask_col).astype(jnp.bfloat16)
    slope = jax.nn.sigmoid(pre)
    dnorm = backward * mask_col * (slope * (1.0 + pre * (1.0 - slope))) * norm_gain
    dinput = rinv * (dnorm - normed * lax.optimization_barrier(jnp.mean(dnorm * normed, axis=-1, keepdims=True)))
    input_grad = (cot_blocks.astype(jnp.float32) + dinput).astype(jnp.bfloat16)
    return (block_output, input_grad, weight_grad)

def reference(features, voxel_mask, cotangent, norm_gain, conv_weight, block_owner):
    limit = math.sqrt(TAPS * C * C)
    outputs = []
    gradients = []
    update = jnp.zeros((TAPS, C, C), jnp.float32)
    for scene_index in range(SCENES):
        owner_row = block_owner[scene_index]
        block_output, input_grad, weight_grad = scene_pass(features[scene_index][owner_row], voxel_mask[scene_index][owner_row], cotangent[scene_index][owner_row], norm_gain, conv_weight)
        outputs.append(jnp.zeros_like(features[scene_index]).at[owner_row].set(block_output))
        gradients.append(jnp.zeros_like(cotangent[scene_index]).at[owner_row].set(input_grad))
        factor = jnp.minimum(1.0, limit / jnp.sqrt(jnp.sum(weight_grad * weight_grad)))
        update = update + factor * weight_grad
    return (jnp.stack(outputs), jnp.stack(gradients), (update / SCENES).reshape(TAPS * C, C))
```

```python
import math

import jax
import jax.numpy as jnp
import numpy as np
from jax import lax
from jax.sharding import PartitionSpec as P

BS = 12
TAPS = 27
GY = 4
GZ = 2


NORM_EPSILON = 1e-06
OFFSETS = [(a, b, c) for a in (-1, 0, 1) for b in (-1, 0, 1) for c in (-1, 0, 1)]
DIRECTIONS = [
    item
    for level in (1, 2, 3)
    for item in OFFSETS
    if abs(item[0]) + abs(item[1]) + abs(item[2]) == level
]
COLUMNS = [(a, b) for a in (-1, 0, 1) for b in (-1, 0, 1)]


def side_range(component, edge):
    if component == 1:
        return (edge - 1, edge)
    if component == -1:
        return (0, 1)
    return (0, edge)


def halo_range(component, edge):
    if component == 1:
        return (edge + 1, edge + 2)
    if component == -1:
        return (0, 1)
    return (1, edge + 1)


def slab_count(direction, edge):
    total = 1
    for component in direction:
        total = total * (1 if component != 0 else edge)
    return total


def row_directions(edge, region_count):
    labels = []
    for position, direction in enumerate(DIRECTIONS):
        labels = labels + [position] * slab_count(direction, edge)
    per_peer = -(-len(labels) // region_count)
    labels = labels + [len(DIRECTIONS)] * (per_peer * region_count - len(labels))
    return (np.array(labels, dtype=np.int32).reshape(per_peer, region_count), len(labels), per_peer)


def holder_table(owner_row, region_count):
    slot_ids = jnp.arange(region_count, dtype=jnp.int32)
    block_of = jnp.sum(
        jnp.where(owner_row[None, :] == slot_ids[:, None], slot_ids[None, :], 0), axis=1
    )
    layer = GY * GZ
    across = region_count // layer
    block_x = block_of // layer
    block_y = block_of // GZ % GY
    block_z = block_of % GZ
    columns = []
    for direction in DIRECTIONS:
        near_x = block_x + direction[0]
        near_y = block_y + direction[1]
        near_z = block_z + direction[2]
        inside = (
            (near_x >= 0)
            & (near_x < across)
            & (near_y >= 0)
            & (near_y < GY)
            & (near_z >= 0)
            & (near_z < GZ)
        )
        target = jnp.clip(near_x * layer + near_y * GZ + near_z, 0, region_count - 1)
        holder = jnp.take(owner_row, target, axis=0)
        columns.append(jnp.where(inside, holder, -1))
    columns.append(jnp.full((region_count,), -1, jnp.int32))
    return jnp.stack(columns, axis=1)


def route_plan(owner_row, region_count):
    labels, padded_rows, per_peer = row_directions(BS, region_count)
    myself = lax.axis_index("region")
    labels_now = lax.dynamic_index_in_dim(jnp.asarray(labels), myself, 1, keepdims=False)
    holders = holder_table(owner_row, region_count)
    sources = jnp.take(holders, labels_now, axis=1)
    valid = sources >= 0
    positions = jnp.arange(per_peer, dtype=jnp.int32)[None, :]
    source_rows = jnp.where(valid, sources * per_peer + positions, 0).reshape(-1)
    return (source_rows, valid.astype(jnp.bfloat16), per_peer)


def dealt_shell(cube, region_count, per_peer):
    edge = cube.shape[0]
    width = cube.shape[3]
    pieces = []
    for direction in DIRECTIONS:
        spans = [side_range(-component, edge) for component in direction]
        pieces.append(
            cube[
                spans[0][0] : spans[0][1], spans[1][0] : spans[1][1], spans[2][0] : spans[2][1]
            ].reshape(-1, width)
        )
    rows = jnp.concatenate(pieces, axis=0)
    rows = jnp.pad(rows, ((0, per_peer * region_count - rows.shape[0]), (0, 0)))
    return rows.reshape(per_peer, region_count, width).transpose(1, 0, 2)


def pick_rows(holdings, plan):
    source_rows, valid, per_peer = plan
    width = holdings.shape[2]
    flat = holdings.reshape(-1, width)
    picked = jnp.take(flat, source_rows, axis=0).reshape(holdings.shape[0], per_peer, width)
    return picked * valid[..., None]


def relay(plan, cube, region_count):
    dealt = lax.all_to_all(
        dealt_shell(cube, region_count, plan[2]), "region", split_axis=0, concat_axis=0, tiled=True
    )
    return lax.all_to_all(pick_rows(dealt, plan), "region", split_axis=0, concat_axis=0, tiled=True)


def assemble(received, cube):
    edge = cube.shape[0]
    width = cube.shape[3]
    whole = received.transpose(1, 0, 2).reshape(-1, width)
    padded = jnp.pad(cube, ((1, 1), (1, 1), (1, 1), (0, 0)))
    offset = 0
    for direction in DIRECTIONS:
        spans = [halo_range(component, edge) for component in direction]
        lengths = [upper - lower for lower, upper in spans]
        count = lengths[0] * lengths[1] * lengths[2]
        piece = whole[offset : offset + count].reshape(lengths[0], lengths[1], lengths[2], width)
        padded = padded.at[
            spans[0][0] : spans[0][1], spans[1][0] : spans[1][1], spans[2][0] : spans[2][1]
        ].set(piece)
        offset = offset + count
    return padded


def column_window(padded, shift_x, shift_y, edge, width):
    column = padded[1 + shift_x : 1 + shift_x + edge, 1 + shift_y : 1 + shift_y + edge]
    return jnp.concatenate(
        [column[:, :, 1 + shift_z : 1 + shift_z + edge] for shift_z in (-1, 0, 1)], axis=-1
    ).reshape(-1, 3 * width)


def convolve(padded_act, padded_grad, grad_block, conv_weight):
    edge = padded_act.shape[0] - 2
    width = padded_act.shape[3]
    forward = jnp.zeros((edge * edge * edge, width), jnp.float32)
    backward = jnp.zeros((edge * edge * edge, width), jnp.float32)
    terms = []
    for group_index, (shift_x, shift_y) in enumerate(COLUMNS):
        group_weight = conv_weight[3 * group_index : 3 * group_index + 3]
        window = column_window(padded_act, shift_x, shift_y, edge, width)
        forward = forward + jnp.dot(
            window, group_weight.reshape(3 * width, width), preferred_element_type=jnp.float32
        )
        mirror_column = padded_grad[
            1 - shift_x : 1 - shift_x + edge, 1 - shift_y : 1 - shift_y + edge
        ]
        mirror = jnp.concatenate(
            [mirror_column[:, :, 1 - shift_z : 1 - shift_z + edge] for shift_z in (-1, 0, 1)],
            axis=-1,
        ).reshape(-1, 3 * width)
        backward = backward + jnp.dot(
            mirror,
            group_weight.transpose(0, 2, 1).reshape(3 * width, width),
            preferred_element_type=jnp.float32,
        )
        terms.append(
            lax.dot_general(
                window, grad_block, (((0,), (0,)), ((), ())), preferred_element_type=jnp.float32
            )
        )
    return (forward, backward, jnp.concatenate(terms, axis=0).reshape(TAPS, width, width))


def body(features, voxel_mask, cotangent, norm_gain, conv_weight, block_owner):
    width = features.shape[-1]
    region_count = lax.axis_size("region")
    plan = route_plan(block_owner[0], region_count)
    inputs = features[0, 0].astype(jnp.float32)
    mask_col = voxel_mask[0, 0].astype(jnp.float32)[:, None]
    rinv = lax.rsqrt(jnp.mean(inputs * inputs, axis=-1, keepdims=True) + NORM_EPSILON)
    normed = inputs * rinv
    pre = normed * norm_gain
    activity = (jax.nn.silu(pre) * mask_col).astype(jnp.bfloat16)
    grad_out = cotangent[0, 0] * voxel_mask[0, 0].astype(jnp.bfloat16)[:, None]
    act_cube = activity.reshape(BS, BS, BS, width)
    grad_cube = grad_out.reshape(BS, BS, BS, width)
    act_recv = relay(plan, act_cube, region_count)
    grad_recv = relay(plan, grad_cube, region_count)
    padded_act = assemble(act_recv, act_cube)
    padded_grad = assemble(grad_recv, grad_cube)
    forward, backward, weight_grad = convolve(padded_act, padded_grad, grad_out, conv_weight)
    block_output = (inputs + forward * mask_col).astype(jnp.bfloat16)
    slope = jax.nn.sigmoid(pre)
    dnorm = backward * mask_col * (slope * (1.0 + pre * (1.0 - slope))) * norm_gain
    dinput = rinv * (dnorm - normed * jnp.mean(dnorm * normed, axis=-1, keepdims=True))
    input_grad = (cotangent[0, 0].astype(jnp.float32) + dinput).astype(jnp.bfloat16)
    flat_grad = weight_grad.reshape(-1, width)
    share_rows = flat_grad.shape[0] // region_count
    limit = math.sqrt(flat_grad.shape[0] * width)
    share = lax.psum_scatter(
        flat_grad.reshape(region_count, share_rows, width), "region", scatter_dimension=0, tiled=True
    ).reshape(share_rows, width)
    total_squares = lax.psum(jnp.sum(share * share), "region")
    factor = jnp.minimum(1.0, limit / jnp.sqrt(total_squares))
    update = lax.psum(share * factor, "scene") / lax.axis_size("scene")
    return (block_output.reshape(features.shape), input_grad.reshape(cotangent.shape), update)


def solution(mesh):
    in_specs = (
        P("scene", "region", None, None),
        P("scene", "region", None),
        P("scene", "region", None, None),
        P(),
        P(),
        P("scene", None),
    )
    out_specs = (
        P("scene", "region", None, None),
        P("scene", "region", None, None),
        P("region", None),
    )
    return jax.shard_map(body, mesh=mesh, in_specs=in_specs, out_specs=out_specs, check_vma=False)
```

```python
import math

import jax
import jax.numpy as jnp
import numpy as np
from jax import lax
from jax.sharding import PartitionSpec as P

BS = 12
TAPS = 27
GY = 4
GZ = 2


NORM_EPSILON = 1e-06
OFFSETS = [(a, b, c) for a in (-1, 0, 1) for b in (-1, 0, 1) for c in (-1, 0, 1)]
DIRECTIONS = [
    item
    for level in (1, 2, 3)
    for item in OFFSETS
    if abs(item[0]) + abs(item[1]) + abs(item[2]) == level
]
COLUMNS = [(a, b) for a in (-1, 0, 1) for b in (-1, 0, 1)]


def side_range(component, edge):
    if component == 1:
        return (edge - 1, edge)
    if component == -1:
        return (0, 1)
    return (0, edge)


def halo_range(component, edge):
    if component == 1:
        return (edge + 1, edge + 2)
    if component == -1:
        return (0, 1)
    return (1, edge + 1)


def slab_count(direction, edge):
    total = 1
    for component in direction:
        total = total * (1 if component != 0 else edge)
    return total


def row_directions(edge, region_count):
    labels = []
    for position, direction in enumerate(DIRECTIONS):
        labels = labels + [position] * slab_count(direction, edge)
    per_peer = -(-len(labels) // region_count)
    labels = labels + [len(DIRECTIONS)] * (per_peer * region_count - len(labels))
    return (np.array(labels, dtype=np.int32).reshape(per_peer, region_count), len(labels), per_peer)


def holder_table(owner_row, region_count):
    slot_ids = jnp.arange(region_count, dtype=jnp.int32)
    block_of = jnp.sum(
        jnp.where(owner_row[None, :] == slot_ids[:, None], slot_ids[None, :], 0), axis=1
    )
    layer = GY * GZ
    across = region_count // layer
    block_x = block_of // layer
    block_y = block_of // GZ % GY
    block_z = block_of % GZ
    columns = []
    for direction in DIRECTIONS:
        near_x = block_x + direction[0]
        near_y = block_y + direction[1]
        near_z = block_z + direction[2]
        inside = (
            (near_x >= 0)
            & (near_x < across)
            & (near_y >= 0)
            & (near_y < GY)
            & (near_z >= 0)
            & (near_z < GZ)
        )
        target = jnp.clip(near_x * layer + near_y * GZ + near_z, 0, region_count - 1)
        holder = jnp.take(owner_row, target, axis=0)
        columns.append(jnp.where(inside, holder, -1))
    columns.append(jnp.full((region_count,), -1, jnp.int32))
    return jnp.stack(columns, axis=1)


def route_plan(owner_row, region_count):
    labels, padded_rows, per_peer = row_directions(BS, region_count)
    myself = lax.axis_index(REGION_AXES)
    labels_now = lax.dynamic_index_in_dim(jnp.asarray(labels), myself, 1, keepdims=False)
    holders = holder_table(owner_row, region_count)
    sources = jnp.take(holders, labels_now, axis=1)
    valid = sources >= 0
    positions = jnp.arange(per_peer, dtype=jnp.int32)[None, :]
    source_rows = jnp.where(valid, sources * per_peer + positions, 0).reshape(-1)
    return (source_rows, valid.astype(jnp.bfloat16), per_peer)


def dealt_shell(cube, region_count, per_peer):
    edge = cube.shape[0]
    width = cube.shape[3]
    pieces = []
    for direction in DIRECTIONS:
        spans = [side_range(-component, edge) for component in direction]
        pieces.append(
            cube[
                spans[0][0] : spans[0][1], spans[1][0] : spans[1][1], spans[2][0] : spans[2][1]
            ].reshape(-1, width)
        )
    rows = jnp.concatenate(pieces, axis=0)
    rows = jnp.pad(rows, ((0, per_peer * region_count - rows.shape[0]), (0, 0)))
    return rows.reshape(per_peer, region_count, width).transpose(1, 0, 2)


def pick_rows(holdings, plan):
    source_rows, valid, per_peer = plan
    width = holdings.shape[2]
    flat = holdings.reshape(-1, width)
    picked = jnp.take(flat, source_rows, axis=0).reshape(holdings.shape[0], per_peer, width)
    return picked * valid[..., None]


def relay(plan, cube, region_count):
    dealt = lax.all_to_all(
        dealt_shell(cube, region_count, plan[2]), REGION_AXES, split_axis=0, concat_axis=0, tiled=True
    )
    return lax.all_to_all(pick_rows(dealt, plan), REGION_AXES, split_axis=0, concat_axis=0, tiled=True)


def assemble(received, cube):
    edge = cube.shape[0]
    width = cube.shape[3]
    whole = received.transpose(1, 0, 2).reshape(-1, width)
    padded = jnp.pad(cube, ((1, 1), (1, 1), (1, 1), (0, 0)))
    offset = 0
    for direction in DIRECTIONS:
        spans = [halo_range(component, edge) for component in direction]
        lengths = [upper - lower for lower, upper in spans]
        count = lengths[0] * lengths[1] * lengths[2]
        piece = whole[offset : offset + count].reshape(lengths[0], lengths[1], lengths[2], width)
        padded = padded.at[
            spans[0][0] : spans[0][1], spans[1][0] : spans[1][1], spans[2][0] : spans[2][1]
        ].set(piece)
        offset = offset + count
    return padded


def column_window(padded, shift_x, shift_y, edge, width):
    column = padded[1 + shift_x : 1 + shift_x + edge, 1 + shift_y : 1 + shift_y + edge]
    return jnp.concatenate(
        [column[:, :, 1 + shift_z : 1 + shift_z + edge] for shift_z in (-1, 0, 1)], axis=-1
    ).reshape(-1, 3 * width)


def convolve(padded_act, padded_grad, grad_block, conv_weight):
    edge = padded_act.shape[0] - 2
    width = padded_act.shape[3]
    forward = jnp.zeros((edge * edge * edge, width), jnp.float32)
    backward = jnp.zeros((edge * edge * edge, width), jnp.float32)
    terms = []
    for group_index, (shift_x, shift_y) in enumerate(COLUMNS):
        group_weight = conv_weight[3 * group_index : 3 * group_index + 3]
        window = column_window(padded_act, shift_x, shift_y, edge, width)
        forward = forward + jnp.dot(
            window, group_weight.reshape(3 * width, width), preferred_element_type=jnp.float32
        )
        mirror_column = padded_grad[
            1 - shift_x : 1 - shift_x + edge, 1 - shift_y : 1 - shift_y + edge
        ]
        mirror = jnp.concatenate(
            [mirror_column[:, :, 1 - shift_z : 1 - shift_z + edge] for shift_z in (-1, 0, 1)],
            axis=-1,
        ).reshape(-1, 3 * width)
        backward = backward + jnp.dot(
            mirror,
            group_weight.transpose(0, 2, 1).reshape(3 * width, width),
            preferred_element_type=jnp.float32,
        )
        terms.append(
            lax.dot_general(
                window, grad_block, (((0,), (0,)), ((), ())), preferred_element_type=jnp.float32
            )
        )
    return (forward, backward, jnp.concatenate(terms, axis=0).reshape(TAPS, width, width))


REGION_AXES = ("z", "y", "core")


def body(features, voxel_mask, cotangent, norm_gain, conv_weight, block_owner):
    width = features.shape[-1]
    region_count = math.prod(lax.axis_size(name) for name in REGION_AXES)
    plan = route_plan(block_owner[0], region_count)
    inputs = features[0, 0].astype(jnp.float32)
    mask_col = voxel_mask[0, 0].astype(jnp.float32)[:, None]
    rinv = lax.rsqrt(jnp.mean(inputs * inputs, axis=-1, keepdims=True) + NORM_EPSILON)
    normed = inputs * rinv
    pre = normed * norm_gain
    activity = (jax.nn.silu(pre) * mask_col).astype(jnp.bfloat16)
    grad_out = cotangent[0, 0] * voxel_mask[0, 0].astype(jnp.bfloat16)[:, None]
    act_cube = activity.reshape(BS, BS, BS, width)
    grad_cube = grad_out.reshape(BS, BS, BS, width)
    act_recv = relay(plan, act_cube, region_count)
    grad_recv = relay(plan, grad_cube, region_count)
    padded_act = assemble(act_recv, act_cube)
    padded_grad = assemble(grad_recv, grad_cube)
    forward, backward, weight_grad = convolve(padded_act, padded_grad, grad_out, conv_weight)
    block_output = (inputs + forward * mask_col).astype(jnp.bfloat16)
    slope = jax.nn.sigmoid(pre)
    dnorm = backward * mask_col * (slope * (1.0 + pre * (1.0 - slope))) * norm_gain
    dinput = rinv * (dnorm - normed * jnp.mean(dnorm * normed, axis=-1, keepdims=True))
    input_grad = (cotangent[0, 0].astype(jnp.float32) + dinput).astype(jnp.bfloat16)
    flat_grad = weight_grad.reshape(-1, width)
    share_rows = flat_grad.shape[0] // region_count
    limit = math.sqrt(flat_grad.shape[0] * width)
    sizes = [lax.axis_size(name) for name in REGION_AXES]
    staged = flat_grad.reshape(*sizes, share_rows, width)
    for position in reversed(range(len(REGION_AXES))):
        staged = staged.reshape(*sizes[: position + 1], share_rows, width)
        staged = lax.psum_scatter(staged, REGION_AXES[position], scatter_dimension=position, tiled=True)
    share = staged.reshape(share_rows, width)
    scene_count = lax.axis_size("scene")
    slots = jnp.arange(scene_count) == lax.axis_index("scene")
    squares = jnp.where(slots, jnp.sum(share * share), 0.0)
    totals = lax.psum(squares, ("scene",) + REGION_AXES)
    total_squares = jnp.sum(jnp.where(slots, totals, 0.0))
    factor = jnp.minimum(1.0, limit / jnp.sqrt(total_squares))
    update = lax.psum(share * factor, "scene") / scene_count
    return (block_output.reshape(features.shape), input_grad.reshape(cotangent.shape), update)


def solution(mesh):
    split = jax.sharding.Mesh(
        mesh.devices.reshape(mesh.shape["scene"], 8, 4, 2), ("scene",) + REGION_AXES
    )
    in_specs = (
        P("scene", REGION_AXES, None, None),
        P("scene", REGION_AXES, None),
        P("scene", REGION_AXES, None, None),
        P(),
        P(),
        P("scene", None),
    )
    out_specs = (
        P("scene", REGION_AXES, None, None),
        P("scene", REGION_AXES, None, None),
        P(REGION_AXES, None),
    )
    return jax.shard_map(body, mesh=split, in_specs=in_specs, out_specs=out_specs, check_vma=False)
```

```python
import math

import jax
import jax.numpy as jnp
import numpy as np
from jax import lax
from jax.sharding import PartitionSpec as P

BS = 12
TAPS = 27
GY = 4
GZ = 2


NORM_EPSILON = 1e-06
OFFSETS = [(a, b, c) for a in (-1, 0, 1) for b in (-1, 0, 1) for c in (-1, 0, 1)]
DIRECTIONS = [
    item
    for level in (1, 2, 3)
    for item in OFFSETS
    if abs(item[0]) + abs(item[1]) + abs(item[2]) == level
]
COLUMNS = [(a, b) for a in (-1, 0, 1) for b in (-1, 0, 1)]


def side_range(component, edge):
    if component == 1:
        return (edge - 1, edge)
    if component == -1:
        return (0, 1)
    return (0, edge)


def halo_range(component, edge):
    if component == 1:
        return (edge + 1, edge + 2)
    if component == -1:
        return (0, 1)
    return (1, edge + 1)


def slab_count(direction, edge):
    total = 1
    for component in direction:
        total = total * (1 if component != 0 else edge)
    return total


def row_directions(edge, region_count):
    labels = []
    for position, direction in enumerate(DIRECTIONS):
        labels = labels + [position] * slab_count(direction, edge)
    per_peer = -(-len(labels) // region_count)
    labels = labels + [len(DIRECTIONS)] * (per_peer * region_count - len(labels))
    return (np.array(labels, dtype=np.int32).reshape(per_peer, region_count), len(labels), per_peer)


def holder_table(owner_row, region_count):
    slot_ids = jnp.arange(region_count, dtype=jnp.int32)
    block_of = jnp.sum(
        jnp.where(owner_row[None, :] == slot_ids[:, None], slot_ids[None, :], 0), axis=1
    )
    layer = GY * GZ
    across = region_count // layer
    block_x = block_of // layer
    block_y = block_of // GZ % GY
    block_z = block_of % GZ
    columns = []
    for direction in DIRECTIONS:
        near_x = block_x + direction[0]
        near_y = block_y + direction[1]
        near_z = block_z + direction[2]
        inside = (
            (near_x >= 0)
            & (near_x < across)
            & (near_y >= 0)
            & (near_y < GY)
            & (near_z >= 0)
            & (near_z < GZ)
        )
        target = jnp.clip(near_x * layer + near_y * GZ + near_z, 0, region_count - 1)
        holder = jnp.take(owner_row, target, axis=0)
        columns.append(jnp.where(inside, holder, -1))
    columns.append(jnp.full((region_count,), -1, jnp.int32))
    return jnp.stack(columns, axis=1)


def route_plan(owner_row, region_count):
    labels, padded_rows, per_peer = row_directions(BS, region_count)
    myself = lax.axis_index(REGION_AXES)
    labels_now = lax.dynamic_index_in_dim(jnp.asarray(labels), myself, 1, keepdims=False)
    holders = holder_table(owner_row, region_count)
    sources = jnp.take(holders, labels_now, axis=1)
    valid = sources >= 0
    positions = jnp.arange(per_peer, dtype=jnp.int32)[None, :]
    source_rows = jnp.where(valid, sources * per_peer + positions, 0).reshape(-1)
    return (source_rows, valid.astype(jnp.bfloat16), per_peer)


def dealt_shell(cube, region_count, per_peer):
    edge = cube.shape[0]
    width = cube.shape[3]
    pieces = []
    for direction in DIRECTIONS:
        spans = [side_range(-component, edge) for component in direction]
        pieces.append(
            cube[
                spans[0][0] : spans[0][1], spans[1][0] : spans[1][1], spans[2][0] : spans[2][1]
            ].reshape(-1, width)
        )
    rows = jnp.concatenate(pieces, axis=0)
    rows = jnp.pad(rows, ((0, per_peer * region_count - rows.shape[0]), (0, 0)))
    return rows.reshape(per_peer, region_count, width).transpose(1, 0, 2)


def pick_rows(holdings, plan):
    source_rows, valid, per_peer = plan
    width = holdings.shape[2]
    flat = holdings.reshape(-1, width)
    picked = jnp.take(flat, source_rows, axis=0).reshape(holdings.shape[0], per_peer, width)
    return picked * valid[..., None]


def relay(plan, cube, region_count):
    dealt = lax.all_to_all(
        dealt_shell(cube, region_count, plan[2]), REGION_AXES, split_axis=0, concat_axis=0, tiled=True
    )
    return lax.all_to_all(pick_rows(dealt, plan), REGION_AXES, split_axis=0, concat_axis=0, tiled=True)


def assemble(received, cube):
    edge = cube.shape[0]
    width = cube.shape[3]
    whole = received.transpose(1, 0, 2).reshape(-1, width)
    padded = jnp.pad(cube, ((1, 1), (1, 1), (1, 1), (0, 0)))
    offset = 0
    for direction in DIRECTIONS:
        spans = [halo_range(component, edge) for component in direction]
        lengths = [upper - lower for lower, upper in spans]
        count = lengths[0] * lengths[1] * lengths[2]
        piece = whole[offset : offset + count].reshape(lengths[0], lengths[1], lengths[2], width)
        padded = padded.at[
            spans[0][0] : spans[0][1], spans[1][0] : spans[1][1], spans[2][0] : spans[2][1]
        ].set(piece)
        offset = offset + count
    return padded


def column_window(padded, shift_x, shift_y, edge, width):
    column = padded[1 + shift_x : 1 + shift_x + edge, 1 + shift_y : 1 + shift_y + edge]
    return jnp.concatenate(
        [column[:, :, 1 + shift_z : 1 + shift_z + edge] for shift_z in (-1, 0, 1)], axis=-1
    ).reshape(-1, 3 * width)


def convolve(padded_act, padded_grad, grad_block, conv_weight):
    edge = padded_act.shape[0] - 2
    width = padded_act.shape[3]
    forward = jnp.zeros((edge * edge * edge, width), jnp.float32)
    backward = jnp.zeros((edge * edge * edge, width), jnp.float32)
    terms = []
    for group_index, (shift_x, shift_y) in enumerate(COLUMNS):
        group_weight = conv_weight[3 * group_index : 3 * group_index + 3]
        window = column_window(padded_act, shift_x, shift_y, edge, width)
        forward = forward + jnp.dot(
            window, group_weight.reshape(3 * width, width), preferred_element_type=jnp.float32
        )
        mirror_column = padded_grad[
            1 - shift_x : 1 - shift_x + edge, 1 - shift_y : 1 - shift_y + edge
        ]
        mirror = jnp.concatenate(
            [mirror_column[:, :, 1 - shift_z : 1 - shift_z + edge] for shift_z in (-1, 0, 1)],
            axis=-1,
        ).reshape(-1, 3 * width)
        backward = backward + jnp.dot(
            mirror,
            group_weight.transpose(0, 2, 1).reshape(3 * width, width),
            preferred_element_type=jnp.float32,
        )
        terms.append(
            lax.dot_general(
                window, grad_block, (((0,), (0,)), ((), ())), preferred_element_type=jnp.float32
            )
        )
    return (forward, backward, jnp.concatenate(terms, axis=0).reshape(TAPS, width, width))


REGION_AXES = ("z", "y", "core")


def butterfly_sum(value, names):
    for name in names:
        size = lax.axis_size(name)
        stride = 1
        while stride < size:
            pairs = [(index, index ^ stride) for index in range(size)]
            value = value + lax.ppermute(value, name, pairs)
            stride = stride * 2
    return value


def body(features, voxel_mask, cotangent, norm_gain, conv_weight, block_owner):
    width = features.shape[-1]
    region_count = math.prod(lax.axis_size(name) for name in REGION_AXES)
    plan = route_plan(block_owner[0], region_count)
    inputs = features[0, 0].astype(jnp.float32)
    mask_col = voxel_mask[0, 0].astype(jnp.float32)[:, None]
    rinv = lax.rsqrt(jnp.mean(inputs * inputs, axis=-1, keepdims=True) + NORM_EPSILON)
    normed = inputs * rinv
    pre = normed * norm_gain
    activity = (jax.nn.silu(pre) * mask_col).astype(jnp.bfloat16)
    grad_out = cotangent[0, 0] * voxel_mask[0, 0].astype(jnp.bfloat16)[:, None]
    act_cube = activity.reshape(BS, BS, BS, width)
    grad_cube = grad_out.reshape(BS, BS, BS, width)
    act_recv = relay(plan, act_cube, region_count)
    grad_recv = relay(plan, grad_cube, region_count)
    padded_act = assemble(act_recv, act_cube)
    padded_grad = assemble(grad_recv, grad_cube)
    forward, backward, weight_grad = convolve(padded_act, padded_grad, grad_out, conv_weight)
    block_output = (inputs + forward * mask_col).astype(jnp.bfloat16)
    slope = jax.nn.sigmoid(pre)
    dnorm = backward * mask_col * (slope * (1.0 + pre * (1.0 - slope))) * norm_gain
    dinput = rinv * (dnorm - normed * jnp.mean(dnorm * normed, axis=-1, keepdims=True))
    input_grad = (cotangent[0, 0].astype(jnp.float32) + dinput).astype(jnp.bfloat16)
    flat_grad = weight_grad.reshape(-1, width)
    share_rows = flat_grad.shape[0] // region_count
    limit = math.sqrt(flat_grad.shape[0] * width)
    sizes = [lax.axis_size(name) for name in REGION_AXES]
    staged = flat_grad.reshape(*sizes, share_rows, width)
    for position in reversed(range(len(REGION_AXES))):
        staged = staged.reshape(*sizes[: position + 1], share_rows, width)
        staged = lax.psum_scatter(staged, REGION_AXES[position], scatter_dimension=position, tiled=True)
    share = staged.reshape(share_rows, width)
    scene_count = lax.axis_size("scene")
    total_squares = butterfly_sum(jnp.sum(share * share), REGION_AXES)
    factor = jnp.minimum(1.0, limit / jnp.sqrt(total_squares))
    update = butterfly_sum(share * factor, ("scene",)) / scene_count
    return (block_output.reshape(features.shape), input_grad.reshape(cotangent.shape), update)


def solution(mesh):
    split = jax.sharding.Mesh(
        mesh.devices.reshape(mesh.shape["scene"], 8, 4, 2), ("scene",) + REGION_AXES
    )
    in_specs = (
        P("scene", REGION_AXES, None, None),
        P("scene", REGION_AXES, None),
        P("scene", REGION_AXES, None, None),
        P(),
        P(),
        P("scene", None),
    )
    out_specs = (
        P("scene", REGION_AXES, None, None),
        P("scene", REGION_AXES, None, None),
        P(REGION_AXES, None),
    )
    return jax.shard_map(body, mesh=split, in_specs=in_specs, out_specs=out_specs, check_vma=False)
```

```python
import math

import jax
import jax.numpy as jnp
import numpy as np
from jax import lax
from jax.sharding import PartitionSpec as P

BS = 12
TAPS = 27
GY = 4
GZ = 2


NORM_EPSILON = 1e-06
OFFSETS = [(a, b, c) for a in (-1, 0, 1) for b in (-1, 0, 1) for c in (-1, 0, 1)]
DIRECTIONS = [
    item
    for level in (1, 2, 3)
    for item in OFFSETS
    if abs(item[0]) + abs(item[1]) + abs(item[2]) == level
]
COLUMNS = [(a, b) for a in (-1, 0, 1) for b in (-1, 0, 1)]


def side_range(component, edge):
    if component == 1:
        return (edge - 1, edge)
    if component == -1:
        return (0, 1)
    return (0, edge)


def halo_range(component, edge):
    if component == 1:
        return (edge + 1, edge + 2)
    if component == -1:
        return (0, 1)
    return (1, edge + 1)


def slab_count(direction, edge):
    total = 1
    for component in direction:
        total = total * (1 if component != 0 else edge)
    return total


def row_directions(edge, region_count):
    labels = []
    for position, direction in enumerate(DIRECTIONS):
        labels = labels + [position] * slab_count(direction, edge)
    per_peer = -(-len(labels) // region_count)
    labels = labels + [len(DIRECTIONS)] * (per_peer * region_count - len(labels))
    return (np.array(labels, dtype=np.int32).reshape(per_peer, region_count), len(labels), per_peer)


def holder_table(owner_row, region_count):
    slot_ids = jnp.arange(region_count, dtype=jnp.int32)
    block_of = jnp.sum(
        jnp.where(owner_row[None, :] == slot_ids[:, None], slot_ids[None, :], 0), axis=1
    )
    layer = GY * GZ
    across = region_count // layer
    block_x = block_of // layer
    block_y = block_of // GZ % GY
    block_z = block_of % GZ
    columns = []
    for direction in DIRECTIONS:
        near_x = block_x + direction[0]
        near_y = block_y + direction[1]
        near_z = block_z + direction[2]
        inside = (
            (near_x >= 0)
            & (near_x < across)
            & (near_y >= 0)
            & (near_y < GY)
            & (near_z >= 0)
            & (near_z < GZ)
        )
        target = jnp.clip(near_x * layer + near_y * GZ + near_z, 0, region_count - 1)
        holder = jnp.take(owner_row, target, axis=0)
        columns.append(jnp.where(inside, holder, -1))
    columns.append(jnp.full((region_count,), -1, jnp.int32))
    return jnp.stack(columns, axis=1)


def route_plan(owner_row, region_count):
    labels, padded_rows, per_peer = row_directions(BS, region_count)
    myself = lax.axis_index(REGION_AXES)
    labels_now = lax.dynamic_index_in_dim(jnp.asarray(labels), myself, 1, keepdims=False)
    holders = holder_table(owner_row, region_count)
    sources = jnp.take(holders, labels_now, axis=1)
    valid = sources >= 0
    positions = jnp.arange(per_peer, dtype=jnp.int32)[None, :]
    source_rows = jnp.where(valid, sources * per_peer + positions, 0).reshape(-1)
    return (source_rows, valid.astype(jnp.bfloat16), per_peer)


def dealt_shell(cube, region_count, per_peer):
    edge = cube.shape[0]
    width = cube.shape[3]
    pieces = []
    for direction in DIRECTIONS:
        spans = [side_range(-component, edge) for component in direction]
        pieces.append(
            cube[
                spans[0][0] : spans[0][1], spans[1][0] : spans[1][1], spans[2][0] : spans[2][1]
            ].reshape(-1, width)
        )
    rows = jnp.concatenate(pieces, axis=0)
    rows = jnp.pad(rows, ((0, per_peer * region_count - rows.shape[0]), (0, 0)))
    return rows.reshape(per_peer, region_count, width).transpose(1, 0, 2)


def pick_rows(holdings, plan):
    source_rows, valid, per_peer = plan
    width = holdings.shape[2]
    flat = holdings.reshape(-1, width)
    picked = jnp.take(flat, source_rows, axis=0).reshape(holdings.shape[0], per_peer, width)
    return picked * valid[..., None]


def relay(plan, cube, region_count):
    dealt = lax.all_to_all(
        dealt_shell(cube, region_count, plan[2]), REGION_AXES, split_axis=0, concat_axis=0, tiled=True
    )
    return lax.all_to_all(pick_rows(dealt, plan), REGION_AXES, split_axis=0, concat_axis=0, tiled=True)


def assemble(received, cube):
    edge = cube.shape[0]
    width = cube.shape[3]
    whole = received.transpose(1, 0, 2).reshape(-1, width)
    padded = jnp.pad(cube, ((1, 1), (1, 1), (1, 1), (0, 0)))
    offset = 0
    for direction in DIRECTIONS:
        spans = [halo_range(component, edge) for component in direction]
        lengths = [upper - lower for lower, upper in spans]
        count = lengths[0] * lengths[1] * lengths[2]
        piece = whole[offset : offset + count].reshape(lengths[0], lengths[1], lengths[2], width)
        padded = padded.at[
            spans[0][0] : spans[0][1], spans[1][0] : spans[1][1], spans[2][0] : spans[2][1]
        ].set(piece)
        offset = offset + count
    return padded


def column_window(padded, shift_x, shift_y, edge, width):
    column = padded[1 + shift_x : 1 + shift_x + edge, 1 + shift_y : 1 + shift_y + edge]
    return jnp.concatenate(
        [column[:, :, 1 + shift_z : 1 + shift_z + edge] for shift_z in (-1, 0, 1)], axis=-1
    ).reshape(-1, 3 * width)


def convolve(padded_act, padded_grad, grad_block, conv_weight):
    edge = padded_act.shape[0] - 2
    width = padded_act.shape[3]
    forward = jnp.zeros((edge * edge * edge, width), jnp.float32)
    backward = jnp.zeros((edge * edge * edge, width), jnp.float32)
    terms = []
    for group_index, (shift_x, shift_y) in enumerate(COLUMNS):
        group_weight = conv_weight[3 * group_index : 3 * group_index + 3]
        window = column_window(padded_act, shift_x, shift_y, edge, width)
        forward = forward + jnp.dot(
            window, group_weight.reshape(3 * width, width), preferred_element_type=jnp.float32
        )
        mirror_column = padded_grad[
            1 - shift_x : 1 - shift_x + edge, 1 - shift_y : 1 - shift_y + edge
        ]
        mirror = jnp.concatenate(
            [mirror_column[:, :, 1 - shift_z : 1 - shift_z + edge] for shift_z in (-1, 0, 1)],
            axis=-1,
        ).reshape(-1, 3 * width)
        backward = backward + jnp.dot(
            mirror,
            group_weight.transpose(0, 2, 1).reshape(3 * width, width),
            preferred_element_type=jnp.float32,
        )
        terms.append(
            lax.dot_general(
                window, grad_block, (((0,), (0,)), ((), ())), preferred_element_type=jnp.float32
            )
        )
    return (forward, backward, jnp.concatenate(terms, axis=0).reshape(TAPS, width, width))


REGION_AXES = ("z", "y", "core")


def butterfly_sum(value, names):
    for name in names:
        size = lax.axis_size(name)
        stride = 1
        while stride < size:
            pairs = [(index, index ^ stride) for index in range(size)]
            value = value + lax.ppermute(value, name, pairs)
            stride = stride * 2
    return value


def body(features, voxel_mask, cotangent, norm_gain, conv_weight, block_owner):
    width = features.shape[-1]
    region_count = math.prod(lax.axis_size(name) for name in REGION_AXES)
    plan = route_plan(block_owner[0], region_count)
    inputs = features[0, 0].astype(jnp.float32)
    mask_col = voxel_mask[0, 0].astype(jnp.float32)[:, None]
    rinv = lax.rsqrt(jnp.mean(inputs * inputs, axis=-1, keepdims=True) + NORM_EPSILON)
    normed = inputs * rinv
    pre = normed * norm_gain
    activity = (jax.nn.silu(pre) * mask_col).astype(jnp.bfloat16)
    grad_out = cotangent[0, 0] * voxel_mask[0, 0].astype(jnp.bfloat16)[:, None]
    act_cube = activity.reshape(BS, BS, BS, width)
    grad_cube = grad_out.reshape(BS, BS, BS, width)
    both_cube = jnp.concatenate([act_cube, grad_cube], axis=-1)
    padded_both = assemble(relay(plan, both_cube, region_count), both_cube)
    padded_act = padded_both[..., :width]
    padded_grad = padded_both[..., width:]
    forward, backward, weight_grad = convolve(padded_act, padded_grad, grad_out, conv_weight)
    block_output = (inputs + forward * mask_col).astype(jnp.bfloat16)
    slope = jax.nn.sigmoid(pre)
    dnorm = backward * mask_col * (slope * (1.0 + pre * (1.0 - slope))) * norm_gain
    dinput = rinv * (dnorm - normed * jnp.mean(dnorm * normed, axis=-1, keepdims=True))
    input_grad = (cotangent[0, 0].astype(jnp.float32) + dinput).astype(jnp.bfloat16)
    flat_grad = weight_grad.reshape(-1, width)
    share_rows = flat_grad.shape[0] // region_count
    limit = math.sqrt(flat_grad.shape[0] * width)
    sizes = [lax.axis_size(name) for name in REGION_AXES]
    staged = flat_grad.reshape(*sizes, share_rows, width)
    for position in reversed(range(len(REGION_AXES))):
        staged = staged.reshape(*sizes[: position + 1], share_rows, width)
        staged = lax.psum_scatter(staged, REGION_AXES[position], scatter_dimension=position, tiled=True)
    share = staged.reshape(share_rows, width)
    scene_count = lax.axis_size("scene")
    total_squares = butterfly_sum(jnp.sum(share * share), REGION_AXES)
    factor = jnp.minimum(1.0, limit / jnp.sqrt(total_squares))
    update = butterfly_sum(share * factor, ("scene",)) / scene_count
    return (block_output.reshape(features.shape), input_grad.reshape(cotangent.shape), update)


def solution(mesh):
    split = jax.sharding.Mesh(
        mesh.devices.reshape(mesh.shape["scene"], 8, 4, 2), ("scene",) + REGION_AXES
    )
    in_specs = (
        P("scene", REGION_AXES, None, None),
        P("scene", REGION_AXES, None),
        P("scene", REGION_AXES, None, None),
        P(),
        P(),
        P("scene", None),
    )
    out_specs = (
        P("scene", REGION_AXES, None, None),
        P("scene", REGION_AXES, None, None),
        P(REGION_AXES, None),
    )
    return jax.shard_map(body, mesh=split, in_specs=in_specs, out_specs=out_specs, check_vma=False)
```

```python
import math

import jax
import jax.numpy as jnp
import numpy as np
from jax import lax
from jax.sharding import PartitionSpec as P

BS = 12
TAPS = 27
GY = 4
GZ = 2


NORM_EPSILON = 1e-06
OFFSETS = [(a, b, c) for a in (-1, 0, 1) for b in (-1, 0, 1) for c in (-1, 0, 1)]
DIRECTIONS = [
    item
    for level in (1, 2, 3)
    for item in OFFSETS
    if abs(item[0]) + abs(item[1]) + abs(item[2]) == level
]
COLUMNS = [(a, b) for a in (-1, 0, 1) for b in (-1, 0, 1)]


def side_range(component, edge):
    if component == 1:
        return (edge - 1, edge)
    if component == -1:
        return (0, 1)
    return (0, edge)


def halo_range(component, edge):
    if component == 1:
        return (edge + 1, edge + 2)
    if component == -1:
        return (0, 1)
    return (1, edge + 1)


def slab_count(direction, edge):
    total = 1
    for component in direction:
        total = total * (1 if component != 0 else edge)
    return total


def row_directions(edge, region_count):
    labels = []
    for position, direction in enumerate(DIRECTIONS):
        labels = labels + [position] * slab_count(direction, edge)
    per_peer = -(-len(labels) // region_count)
    labels = labels + [len(DIRECTIONS)] * (per_peer * region_count - len(labels))
    return (np.array(labels, dtype=np.int32).reshape(per_peer, region_count), len(labels), per_peer)


def holder_table(owner_row, region_count):
    slot_ids = jnp.arange(region_count, dtype=jnp.int32)
    block_of = jnp.sum(
        jnp.where(owner_row[None, :] == slot_ids[:, None], slot_ids[None, :], 0), axis=1
    )
    layer = GY * GZ
    across = region_count // layer
    block_x = block_of // layer
    block_y = block_of // GZ % GY
    block_z = block_of % GZ
    columns = []
    for direction in DIRECTIONS:
        near_x = block_x + direction[0]
        near_y = block_y + direction[1]
        near_z = block_z + direction[2]
        inside = (
            (near_x >= 0)
            & (near_x < across)
            & (near_y >= 0)
            & (near_y < GY)
            & (near_z >= 0)
            & (near_z < GZ)
        )
        target = jnp.clip(near_x * layer + near_y * GZ + near_z, 0, region_count - 1)
        holder = jnp.take(owner_row, target, axis=0)
        columns.append(jnp.where(inside, holder, -1))
    columns.append(jnp.full((region_count,), -1, jnp.int32))
    return jnp.stack(columns, axis=1)


def route_plan(owner_row, region_count):
    labels, padded_rows, per_peer = row_directions(BS, region_count)
    myself = lax.axis_index(REGION_AXES)
    labels_now = lax.dynamic_index_in_dim(jnp.asarray(labels), myself, 1, keepdims=False)
    holders = holder_table(owner_row, region_count)
    sources = jnp.take(holders, labels_now, axis=1)
    valid = sources >= 0
    positions = jnp.arange(per_peer, dtype=jnp.int32)[None, :]
    source_rows = jnp.where(valid, sources * per_peer + positions, 0).reshape(-1)
    return (source_rows, valid.astype(jnp.bfloat16), per_peer)


def dealt_shell(cube, region_count, per_peer):
    edge = cube.shape[0]
    width = cube.shape[3]
    pieces = []
    for direction in DIRECTIONS:
        spans = [side_range(-component, edge) for component in direction]
        pieces.append(
            cube[
                spans[0][0] : spans[0][1], spans[1][0] : spans[1][1], spans[2][0] : spans[2][1]
            ].reshape(-1, width)
        )
    rows = jnp.concatenate(pieces, axis=0)
    rows = jnp.pad(rows, ((0, per_peer * region_count - rows.shape[0]), (0, 0)))
    return rows.reshape(per_peer, region_count, width).transpose(1, 0, 2)


def pick_rows(holdings, plan):
    source_rows, valid, per_peer = plan
    width = holdings.shape[2]
    flat = holdings.reshape(-1, width)
    picked = jnp.take(flat, source_rows, axis=0).reshape(holdings.shape[0], per_peer, width)
    return picked * valid[..., None]


def relay(plan, cube, region_count):
    dealt = lax.all_to_all(
        dealt_shell(cube, region_count, plan[2]), REGION_AXES, split_axis=0, concat_axis=0, tiled=True
    )
    return lax.all_to_all(pick_rows(dealt, plan), REGION_AXES, split_axis=0, concat_axis=0, tiled=True)


def assemble(received, cube):
    edge = cube.shape[0]
    width = cube.shape[3]
    whole = received.transpose(1, 0, 2).reshape(-1, width)
    padded = jnp.pad(cube, ((1, 1), (1, 1), (1, 1), (0, 0)))
    offset = 0
    for direction in DIRECTIONS:
        spans = [halo_range(component, edge) for component in direction]
        lengths = [upper - lower for lower, upper in spans]
        count = lengths[0] * lengths[1] * lengths[2]
        piece = whole[offset : offset + count].reshape(lengths[0], lengths[1], lengths[2], width)
        padded = padded.at[
            spans[0][0] : spans[0][1], spans[1][0] : spans[1][1], spans[2][0] : spans[2][1]
        ].set(piece)
        offset = offset + count
    return padded


def column_window(padded, shift_x, shift_y, edge, width):
    column = padded[1 + shift_x : 1 + shift_x + edge, 1 + shift_y : 1 + shift_y + edge]
    return jnp.concatenate(
        [column[:, :, 1 + shift_z : 1 + shift_z + edge] for shift_z in (-1, 0, 1)], axis=-1
    ).reshape(-1, 3 * width)


def convolve(padded_act, padded_grad, grad_block, conv_weight):
    edge = padded_act.shape[0] - 2
    width = padded_act.shape[3]
    forward = jnp.zeros((edge * edge * edge, width), jnp.float32)
    backward = jnp.zeros((edge * edge * edge, width), jnp.float32)
    terms = []
    for group_index, (shift_x, shift_y) in enumerate(COLUMNS):
        group_weight = conv_weight[3 * group_index : 3 * group_index + 3]
        window = column_window(padded_act, shift_x, shift_y, edge, width)
        forward = forward + jnp.dot(
            window, group_weight.reshape(3 * width, width), preferred_element_type=jnp.float32
        )
        mirror_column = padded_grad[
            1 - shift_x : 1 - shift_x + edge, 1 - shift_y : 1 - shift_y + edge
        ]
        mirror = jnp.concatenate(
            [mirror_column[:, :, 1 - shift_z : 1 - shift_z + edge] for shift_z in (-1, 0, 1)],
            axis=-1,
        ).reshape(-1, 3 * width)
        backward = backward + jnp.dot(
            mirror,
            group_weight.transpose(0, 2, 1).reshape(3 * width, width),
            preferred_element_type=jnp.float32,
        )
        terms.append(
            lax.dot_general(
                window, grad_block, (((0,), (0,)), ((), ())), preferred_element_type=jnp.float32
            )
        )
    return (forward, backward, jnp.concatenate(terms, axis=0).reshape(TAPS, width, width))


REGION_AXES = ("z", "y", "core")


def direct_scatter_sum(blocks, name, axis):
    size = lax.axis_size(name)
    me = lax.axis_index(name)
    total = lax.dynamic_index_in_dim(blocks, me, axis, keepdims=False)
    for shift in range(1, size):
        piece = lax.dynamic_index_in_dim(blocks, (me + shift) % size, axis, keepdims=False)
        pairs = [(index, (index + shift) % size) for index in range(size)]
        total = total + lax.ppermute(piece, name, pairs)
    return total


def direct_sum(value, names):
    for name in names:
        size = lax.axis_size(name)
        received = [
            lax.ppermute(value, name, [(index, (index + shift) % size) for index in range(size)])
            for shift in range(1, size)
        ]
        for piece in received:
            value = value + piece
    return value


def butterfly_sum(value, names):
    for name in names:
        size = lax.axis_size(name)
        stride = 1
        while stride < size:
            pairs = [(index, index ^ stride) for index in range(size)]
            value = value + lax.ppermute(value, name, pairs)
            stride = stride * 2
    return value


def body(features, voxel_mask, cotangent, norm_gain, conv_weight, block_owner):
    width = features.shape[-1]
    region_count = math.prod(lax.axis_size(name) for name in REGION_AXES)
    plan = route_plan(block_owner[0], region_count)
    inputs = features[0, 0].astype(jnp.float32)
    mask_col = voxel_mask[0, 0].astype(jnp.float32)[:, None]
    rinv = lax.rsqrt(jnp.mean(inputs * inputs, axis=-1, keepdims=True) + NORM_EPSILON)
    normed = inputs * rinv
    pre = normed * norm_gain
    activity = (jax.nn.silu(pre) * mask_col).astype(jnp.bfloat16)
    grad_out = cotangent[0, 0] * voxel_mask[0, 0].astype(jnp.bfloat16)[:, None]
    act_cube = activity.reshape(BS, BS, BS, width)
    grad_cube = grad_out.reshape(BS, BS, BS, width)
    both_cube = jnp.concatenate([act_cube, grad_cube], axis=-1)
    padded_both = assemble(relay(plan, both_cube, region_count), both_cube)
    padded_act = padded_both[..., :width]
    padded_grad = padded_both[..., width:]
    forward, backward, weight_grad = convolve(padded_act, padded_grad, grad_out, conv_weight)
    block_output = (inputs + forward * mask_col).astype(jnp.bfloat16)
    slope = jax.nn.sigmoid(pre)
    dnorm = backward * mask_col * (slope * (1.0 + pre * (1.0 - slope))) * norm_gain
    dinput = rinv * (dnorm - normed * jnp.mean(dnorm * normed, axis=-1, keepdims=True))
    input_grad = (cotangent[0, 0].astype(jnp.float32) + dinput).astype(jnp.bfloat16)
    flat_grad = weight_grad.reshape(-1, width)
    share_rows = flat_grad.shape[0] // region_count
    limit = math.sqrt(flat_grad.shape[0] * width)
    sizes = [lax.axis_size(name) for name in REGION_AXES]
    staged = lax.psum_scatter(
        flat_grad.reshape(*sizes, share_rows, width), REGION_AXES[-1], scatter_dimension=2, tiled=True
    ).reshape(*sizes[:2], share_rows, width)
    staged = direct_scatter_sum(staged, REGION_AXES[1], 1)
    share = direct_scatter_sum(staged, REGION_AXES[0], 0)
    scene_count = lax.axis_size("scene")
    total_squares = direct_sum(jnp.sum(share * share), REGION_AXES)
    factor = jnp.minimum(1.0, limit / jnp.sqrt(total_squares))
    update = butterfly_sum(share * factor, ("scene",)) / scene_count
    return (block_output.reshape(features.shape), input_grad.reshape(cotangent.shape), update)


def solution(mesh):
    split = jax.sharding.Mesh(
        mesh.devices.reshape(mesh.shape["scene"], 8, 4, 2), ("scene",) + REGION_AXES
    )
    in_specs = (
        P("scene", REGION_AXES, None, None),
        P("scene", REGION_AXES, None),
        P("scene", REGION_AXES, None, None),
        P(),
        P(),
        P("scene", None),
    )
    out_specs = (
        P("scene", REGION_AXES, None, None),
        P("scene", REGION_AXES, None, None),
        P(REGION_AXES, None),
    )
    return jax.shard_map(body, mesh=split, in_specs=in_specs, out_specs=out_specs, check_vma=False)
```

```python
import math

import jax
import jax.numpy as jnp
import numpy as np
from jax import lax
from jax.sharding import PartitionSpec as P

BS = 12
TAPS = 27
GY = 4
GZ = 2


NORM_EPSILON = 1e-06
OFFSETS = [(a, b, c) for a in (-1, 0, 1) for b in (-1, 0, 1) for c in (-1, 0, 1)]
DIRECTIONS = [
    item
    for level in (1, 2, 3)
    for item in OFFSETS
    if abs(item[0]) + abs(item[1]) + abs(item[2]) == level
]
COLUMNS = [(a, b) for a in (-1, 0, 1) for b in (-1, 0, 1)]


def side_range(component, edge):
    if component == 1:
        return (edge - 1, edge)
    if component == -1:
        return (0, 1)
    return (0, edge)


def halo_range(component, edge):
    if component == 1:
        return (edge + 1, edge + 2)
    if component == -1:
        return (0, 1)
    return (1, edge + 1)


def slab_count(direction, edge):
    total = 1
    for component in direction:
        total = total * (1 if component != 0 else edge)
    return total


def row_directions(edge, region_count):
    labels = []
    for position, direction in enumerate(DIRECTIONS):
        labels = labels + [position] * slab_count(direction, edge)
    per_peer = -(-len(labels) // region_count)
    labels = labels + [len(DIRECTIONS)] * (per_peer * region_count - len(labels))
    return (np.array(labels, dtype=np.int32).reshape(per_peer, region_count), len(labels), per_peer)


def holder_table(owner_row, region_count):
    slot_ids = jnp.arange(region_count, dtype=jnp.int32)
    block_of = jnp.sum(
        jnp.where(owner_row[None, :] == slot_ids[:, None], slot_ids[None, :], 0), axis=1
    )
    layer = GY * GZ
    across = region_count // layer
    block_x = block_of // layer
    block_y = block_of // GZ % GY
    block_z = block_of % GZ
    columns = []
    for direction in DIRECTIONS:
        near_x = block_x + direction[0]
        near_y = block_y + direction[1]
        near_z = block_z + direction[2]
        inside = (
            (near_x >= 0)
            & (near_x < across)
            & (near_y >= 0)
            & (near_y < GY)
            & (near_z >= 0)
            & (near_z < GZ)
        )
        target = jnp.clip(near_x * layer + near_y * GZ + near_z, 0, region_count - 1)
        holder = jnp.take(owner_row, target, axis=0)
        columns.append(jnp.where(inside, holder, -1))
    columns.append(jnp.full((region_count,), -1, jnp.int32))
    return jnp.stack(columns, axis=1)


def route_plan(owner_row, region_count):
    labels, padded_rows, per_peer = row_directions(BS, region_count)
    myself = lax.axis_index(REGION_AXES)
    labels_now = lax.dynamic_index_in_dim(jnp.asarray(labels), myself, 1, keepdims=False)
    holders = holder_table(owner_row, region_count)
    sources = jnp.take(holders, labels_now, axis=1)
    valid = sources >= 0
    positions = jnp.arange(per_peer, dtype=jnp.int32)[None, :]
    source_rows = jnp.where(valid, sources * per_peer + positions, 0).reshape(-1)
    return (source_rows, valid.astype(jnp.bfloat16), per_peer)


def pick_rows(holdings, plan):
    source_rows, valid, per_peer = plan
    width = holdings.shape[2]
    flat = holdings.reshape(-1, width)
    picked = jnp.take(flat, source_rows, axis=0).reshape(holdings.shape[0], per_peer, width)
    return picked * valid[..., None]


def shell_index(edge, region_count, per_peer):
    cube_ids = np.arange(edge * edge * edge).reshape(edge, edge, edge)
    pieces = []
    for direction in DIRECTIONS:
        spans = [side_range(-component, edge) for component in direction]
        pieces.append(
            cube_ids[
                spans[0][0] : spans[0][1], spans[1][0] : spans[1][1], spans[2][0] : spans[2][1]
            ].reshape(-1)
        )
    rows = np.concatenate(pieces)
    rows = np.pad(rows, (0, per_peer * region_count - rows.size))
    return rows.reshape(per_peer, region_count).T.reshape(-1).astype(np.int32)


def assemble_index(edge, region_count, per_peer):
    side = edge + 2
    inner = edge * edge * edge
    table = np.zeros((side, side, side), np.int64)
    table[1 : edge + 1, 1 : edge + 1, 1 : edge + 1] = np.arange(inner).reshape(edge, edge, edge)
    offset = 0
    for direction in DIRECTIONS:
        spans = [halo_range(component, edge) for component in direction]
        lengths = [upper - lower for lower, upper in spans]
        count = lengths[0] * lengths[1] * lengths[2]
        whole_rows = offset + np.arange(count)
        sources = inner + (whole_rows % region_count) * per_peer + whole_rows // region_count
        table[
            spans[0][0] : spans[0][1], spans[1][0] : spans[1][1], spans[2][0] : spans[2][1]
        ] = sources.reshape(lengths)
        offset = offset + count
    return table.reshape(-1).astype(np.int32)


def dealt_rows(cube, region_count, per_peer):
    width = cube.shape[3]
    index = shell_index(cube.shape[0], region_count, per_peer)
    picked = jnp.take(cube.reshape(-1, width), index, axis=0, mode="clip")
    return picked.reshape(region_count, per_peer, width)


def assemble_rows(received, cube):
    width = cube.shape[3]
    index = assemble_index(cube.shape[0], received.shape[0], received.shape[1])
    source = jnp.concatenate([cube.reshape(-1, width), received.reshape(-1, width)], axis=0)
    return jnp.take(source, index, axis=0, mode="clip")


def relay(plan, cube, region_count):
    dealt = lax.all_to_all(
        dealt_rows(cube, region_count, plan[2]), REGION_AXES, split_axis=0, concat_axis=0, tiled=True
    )
    return lax.all_to_all(pick_rows(dealt, plan), REGION_AXES, split_axis=0, concat_axis=0, tiled=True)


REGION_AXES = ("z", "y", "core")


def direct_scatter_sum(blocks, name, axis):
    size = lax.axis_size(name)
    me = lax.axis_index(name)
    total = lax.dynamic_index_in_dim(blocks, me, axis, keepdims=False)
    for shift in range(1, size):
        piece = lax.dynamic_index_in_dim(blocks, (me + shift) % size, axis, keepdims=False)
        pairs = [(index, (index + shift) % size) for index in range(size)]
        total = total + lax.ppermute(piece, name, pairs)
    return total


def direct_sum(value, names):
    for name in names:
        size = lax.axis_size(name)
        received = [
            lax.ppermute(value, name, [(index, (index + shift) % size) for index in range(size)])
            for shift in range(1, size)
        ]
        for piece in received:
            value = value + piece
    return value


def butterfly_sum(value, names):
    for name in names:
        size = lax.axis_size(name)
        stride = 1
        while stride < size:
            pairs = [(index, index ^ stride) for index in range(size)]
            value = value + lax.ppermute(value, name, pairs)
            stride = stride * 2
    return value


def convolve_flat(flat, edge, grad_block, conv_weight):
    side = edge + 2
    width = grad_block.shape[1]
    plane = side * side
    base = plane + side + 1
    span = (edge - 1) * plane + (edge - 1) * side + edge
    zero_row = jnp.zeros((1, 2 * width), flat.dtype)
    after = jnp.concatenate([flat[1:], zero_row], axis=0)
    before = jnp.concatenate([zero_row, flat[:-1]], axis=0)
    act_rows = jnp.concatenate([before[:, :width], flat[:, :width], after[:, :width]], axis=1)
    grad_rows = jnp.concatenate([after[:, width:], flat[:, width:], before[:, width:]], axis=1)
    own = jnp.pad(grad_block.reshape(edge, edge, edge, width), ((1, 1), (1, 1), (1, 1), (0, 0)))
    own = own.reshape(-1, width)[base : base + span]
    forward = jnp.zeros((span, width), jnp.float32)
    backward = jnp.zeros((span, width), jnp.float32)
    terms = []
    for group_index, (shift_x, shift_y) in enumerate(COLUMNS):
        group_weight = conv_weight[3 * group_index : 3 * group_index + 3]
        start = base + shift_x * plane + shift_y * side
        window = act_rows[start : start + span]
        forward = forward + jnp.dot(
            window, group_weight.reshape(3 * width, width), preferred_element_type=jnp.float32
        )
        mirror_start = base - shift_x * plane - shift_y * side
        mirror = grad_rows[mirror_start : mirror_start + span]
        backward = backward + jnp.dot(
            mirror,
            group_weight.transpose(0, 2, 1).reshape(3 * width, width),
            preferred_element_type=jnp.float32,
        )
        terms.append(
            lax.dot_general(window, own, (((0,), (0,)), ((), ())), preferred_element_type=jnp.float32)
        )

    def interior(rows):
        rows = jnp.pad(rows, ((0, edge * plane - span), (0, 0)))
        return rows.reshape(edge, side, side, width)[:, :edge, :edge].reshape(-1, width)

    return (interior(forward), interior(backward), jnp.concatenate(terms, axis=0).reshape(TAPS, width, width))


def body(features, voxel_mask, cotangent, norm_gain, conv_weight, block_owner):
    width = features.shape[-1]
    region_count = math.prod(lax.axis_size(name) for name in REGION_AXES)
    plan = route_plan(block_owner[0], region_count)
    inputs = features[0, 0].astype(jnp.float32)
    mask_col = voxel_mask[0, 0].astype(jnp.float32)[:, None]
    rinv = lax.rsqrt(jnp.mean(inputs * inputs, axis=-1, keepdims=True) + NORM_EPSILON)
    normed = inputs * rinv
    pre = normed * norm_gain
    activity = (jax.nn.silu(pre) * mask_col).astype(jnp.bfloat16)
    grad_out = cotangent[0, 0] * voxel_mask[0, 0].astype(jnp.bfloat16)[:, None]
    act_cube = activity.reshape(BS, BS, BS, width)
    grad_cube = grad_out.reshape(BS, BS, BS, width)
    both_cube = jnp.concatenate([act_cube, grad_cube], axis=-1)
    flat_both = assemble_rows(relay(plan, both_cube, region_count), both_cube)
    forward, backward, weight_grad = convolve_flat(flat_both, BS, grad_out, conv_weight)
    block_output = (inputs + forward * mask_col).astype(jnp.bfloat16)
    slope = jax.nn.sigmoid(pre)
    dnorm = backward * mask_col * (slope * (1.0 + pre * (1.0 - slope))) * norm_gain
    dinput = rinv * (dnorm - normed * jnp.mean(dnorm * normed, axis=-1, keepdims=True))
    input_grad = (cotangent[0, 0].astype(jnp.float32) + dinput).astype(jnp.bfloat16)
    flat_grad = weight_grad.reshape(-1, width)
    share_rows = flat_grad.shape[0] // region_count
    limit = math.sqrt(flat_grad.shape[0] * width)
    sizes = [lax.axis_size(name) for name in REGION_AXES]
    staged = lax.psum_scatter(
        flat_grad.reshape(*sizes, share_rows, width), REGION_AXES[-1], scatter_dimension=2, tiled=True
    ).reshape(*sizes[:2], share_rows, width)
    staged = direct_scatter_sum(staged, REGION_AXES[1], 1)
    share = direct_scatter_sum(staged, REGION_AXES[0], 0)
    scene_count = lax.axis_size("scene")
    total_squares = direct_sum(jnp.sum(share * share), REGION_AXES)
    factor = jnp.minimum(1.0, limit / jnp.sqrt(total_squares))
    update = butterfly_sum(share * factor, ("scene",)) / scene_count
    return (block_output.reshape(features.shape), input_grad.reshape(cotangent.shape), update)


def solution(mesh):
    split = jax.sharding.Mesh(
        mesh.devices.reshape(mesh.shape["scene"], 8, 4, 2), ("scene",) + REGION_AXES
    )
    in_specs = (
        P("scene", REGION_AXES, None, None),
        P("scene", REGION_AXES, None),
        P("scene", REGION_AXES, None, None),
        P(),
        P(),
        P("scene", None),
    )
    out_specs = (
        P("scene", REGION_AXES, None, None),
        P("scene", REGION_AXES, None, None),
        P(REGION_AXES, None),
    )
    return jax.shard_map(body, mesh=split, in_specs=in_specs, out_specs=out_specs, check_vma=False)
```

```python
import math

import jax
import jax.numpy as jnp
import numpy as np
from jax import lax
from jax.sharding import PartitionSpec as P

BS = 12
TAPS = 27
GY = 4
GZ = 2


NORM_EPSILON = 1e-06
OFFSETS = [(a, b, c) for a in (-1, 0, 1) for b in (-1, 0, 1) for c in (-1, 0, 1)]
DIRECTIONS = [
    item
    for level in (1, 2, 3)
    for item in OFFSETS
    if abs(item[0]) + abs(item[1]) + abs(item[2]) == level
]
COLUMNS = [(a, b) for a in (-1, 0, 1) for b in (-1, 0, 1)]


def side_range(component, edge):
    if component == 1:
        return (edge - 1, edge)
    if component == -1:
        return (0, 1)
    return (0, edge)


def halo_range(component, edge):
    if component == 1:
        return (edge + 1, edge + 2)
    if component == -1:
        return (0, 1)
    return (1, edge + 1)


def slab_count(direction, edge):
    total = 1
    for component in direction:
        total = total * (1 if component != 0 else edge)
    return total


def row_directions(edge, region_count):
    labels = []
    for position, direction in enumerate(DIRECTIONS):
        labels = labels + [position] * slab_count(direction, edge)
    per_peer = -(-len(labels) // region_count)
    labels = labels + [len(DIRECTIONS)] * (per_peer * region_count - len(labels))
    return (np.array(labels, dtype=np.int32).reshape(per_peer, region_count), len(labels), per_peer)


def holder_table(owner_row, region_count):
    slot_ids = jnp.arange(region_count, dtype=jnp.int32)
    block_of = jnp.sum(
        jnp.where(owner_row[None, :] == slot_ids[:, None], slot_ids[None, :], 0), axis=1
    )
    layer = GY * GZ
    across = region_count // layer
    steps = np.array(DIRECTIONS, dtype=np.int32)
    near_x = (block_of // layer)[:, None] + steps[None, :, 0]
    near_y = (block_of // GZ % GY)[:, None] + steps[None, :, 1]
    near_z = (block_of % GZ)[:, None] + steps[None, :, 2]
    inside = (
        (near_x >= 0)
        & (near_x < across)
        & (near_y >= 0)
        & (near_y < GY)
        & (near_z >= 0)
        & (near_z < GZ)
    )
    target = jnp.clip(near_x * layer + near_y * GZ + near_z, 0, region_count - 1)
    holder = jnp.take(owner_row, target.reshape(-1), axis=0).reshape(target.shape)
    columns = jnp.where(inside, holder, -1)
    return jnp.concatenate([columns, jnp.full((region_count, 1), -1, jnp.int32)], axis=1)


def route_plan(owner_row, region_count):
    labels, padded_rows, per_peer = row_directions(BS, region_count)
    myself = lax.axis_index(REGION_AXES)
    labels_now = lax.dynamic_index_in_dim(jnp.asarray(labels), myself, 1, keepdims=False)
    holders = holder_table(owner_row, region_count)
    sources = jnp.take(holders, labels_now, axis=1)
    valid = sources >= 0
    positions = jnp.arange(per_peer, dtype=jnp.int32)[None, :]
    source_rows = jnp.where(valid, sources * per_peer + positions, 0).reshape(-1)
    return (source_rows, valid.astype(jnp.bfloat16), per_peer)


def pick_rows(holdings, plan):
    source_rows, valid, per_peer = plan
    width = holdings.shape[2]
    flat = holdings.reshape(-1, width)
    picked = jnp.take(flat, source_rows, axis=0).reshape(holdings.shape[0], per_peer, width)
    return picked * valid[..., None]


def shell_index(edge, region_count, per_peer):
    cube_ids = np.arange(edge * edge * edge).reshape(edge, edge, edge)
    pieces = []
    for direction in DIRECTIONS:
        spans = [side_range(-component, edge) for component in direction]
        pieces.append(
            cube_ids[
                spans[0][0] : spans[0][1], spans[1][0] : spans[1][1], spans[2][0] : spans[2][1]
            ].reshape(-1)
        )
    rows = np.concatenate(pieces)
    rows = np.pad(rows, (0, per_peer * region_count - rows.size))
    return rows.reshape(per_peer, region_count).T.reshape(-1).astype(np.int32)


def assemble_index(edge, region_count, per_peer):
    side = edge + 2
    inner = edge * edge * edge
    table = np.zeros((side, side, side), np.int64)
    table[1 : edge + 1, 1 : edge + 1, 1 : edge + 1] = np.arange(inner).reshape(edge, edge, edge)
    offset = 0
    for direction in DIRECTIONS:
        spans = [halo_range(component, edge) for component in direction]
        lengths = [upper - lower for lower, upper in spans]
        count = lengths[0] * lengths[1] * lengths[2]
        whole_rows = offset + np.arange(count)
        sources = inner + (whole_rows % region_count) * per_peer + whole_rows // region_count
        table[
            spans[0][0] : spans[0][1], spans[1][0] : spans[1][1], spans[2][0] : spans[2][1]
        ] = sources.reshape(lengths)
        offset = offset + count
    return table.reshape(-1).astype(np.int32)


def dealt_rows(cube, region_count, per_peer):
    width = cube.shape[3]
    index = shell_index(cube.shape[0], region_count, per_peer)
    picked = jnp.take(cube.reshape(-1, width), index, axis=0, mode="clip")
    return picked.reshape(region_count, per_peer, width)


def assemble_rows(received, cube):
    width = cube.shape[3]
    index = assemble_index(cube.shape[0], received.shape[0], received.shape[1])
    source = jnp.concatenate([cube.reshape(-1, width), received.reshape(-1, width)], axis=0)
    return jnp.take(source, index, axis=0, mode="clip")


def relay(plan, cube, region_count):
    dealt = lax.all_to_all(
        dealt_rows(cube, region_count, plan[2]), REGION_AXES, split_axis=0, concat_axis=0, tiled=True
    )
    return lax.all_to_all(pick_rows(dealt, plan), REGION_AXES, split_axis=0, concat_axis=0, tiled=True)


REGION_AXES = ("z", "y", "core")


def direct_scatter_sum(blocks, name, axis):
    size = lax.axis_size(name)
    me = lax.axis_index(name)
    total = lax.dynamic_index_in_dim(blocks, me, axis, keepdims=False)
    for shift in range(1, size):
        piece = lax.dynamic_index_in_dim(blocks, (me + shift) % size, axis, keepdims=False)
        pairs = [(index, (index + shift) % size) for index in range(size)]
        total = total + lax.ppermute(piece, name, pairs)
    return total


def direct_sum(value, names):
    for name in names:
        size = lax.axis_size(name)
        received = [
            lax.ppermute(value, name, [(index, (index + shift) % size) for index in range(size)])
            for shift in range(1, size)
        ]
        for piece in received:
            value = value + piece
    return value


def butterfly_sum(value, names):
    for name in names:
        size = lax.axis_size(name)
        stride = 1
        while stride < size:
            pairs = [(index, index ^ stride) for index in range(size)]
            value = value + lax.ppermute(value, name, pairs)
            stride = stride * 2
    return value


def convolve_flat(flat, edge, grad_block, conv_weight):
    side = edge + 2
    width = grad_block.shape[1]
    plane = side * side
    base = plane + side + 1
    span = (edge - 1) * plane + (edge - 1) * side + edge
    zero_row = jnp.zeros((1, 2 * width), flat.dtype)
    after = jnp.concatenate([flat[1:], zero_row], axis=0)
    before = jnp.concatenate([zero_row, flat[:-1]], axis=0)
    act_rows = jnp.concatenate([before[:, :width], flat[:, :width], after[:, :width]], axis=1)
    grad_rows = jnp.concatenate([after[:, width:], flat[:, width:], before[:, width:]], axis=1)
    own = jnp.pad(grad_block.reshape(edge, edge, edge, width), ((1, 1), (1, 1), (1, 1), (0, 0)))
    own = own.reshape(-1, width)[base : base + span]
    forward = jnp.zeros((span, width), jnp.float32)
    backward = jnp.zeros((span, width), jnp.float32)
    terms = []
    for group_index, (shift_x, shift_y) in enumerate(COLUMNS):
        group_weight = conv_weight[3 * group_index : 3 * group_index + 3]
        start = base + shift_x * plane + shift_y * side
        window = act_rows[start : start + span]
        forward = forward + jnp.dot(
            window, group_weight.reshape(3 * width, width), preferred_element_type=jnp.float32
        )
        mirror_start = base - shift_x * plane - shift_y * side
        mirror = grad_rows[mirror_start : mirror_start + span]
        backward = backward + jnp.dot(
            mirror,
            group_weight.transpose(0, 2, 1).reshape(3 * width, width),
            preferred_element_type=jnp.float32,
        )
        terms.append(
            lax.dot_general(window, own, (((0,), (0,)), ((), ())), preferred_element_type=jnp.float32)
        )

    def interior(rows):
        rows = jnp.pad(rows, ((0, edge * plane - span), (0, 0)))
        return rows.reshape(edge, side, side, width)[:, :edge, :edge].reshape(-1, width)

    return (interior(forward), interior(backward), jnp.concatenate(terms, axis=0).reshape(TAPS, width, width))


def body(features, voxel_mask, cotangent, norm_gain, conv_weight, block_owner):
    width = features.shape[-1]
    region_count = math.prod(lax.axis_size(name) for name in REGION_AXES)
    plan = route_plan(block_owner[0], region_count)
    inputs = features[0, 0].astype(jnp.float32)
    mask_col = voxel_mask[0, 0].astype(jnp.float32)[:, None]
    rinv = lax.rsqrt(jnp.mean(inputs * inputs, axis=-1, keepdims=True) + NORM_EPSILON)
    normed = inputs * rinv
    pre = normed * norm_gain
    activity = (jax.nn.silu(pre) * mask_col).astype(jnp.bfloat16)
    grad_out = cotangent[0, 0] * voxel_mask[0, 0].astype(jnp.bfloat16)[:, None]
    act_cube = activity.reshape(BS, BS, BS, width)
    grad_cube = grad_out.reshape(BS, BS, BS, width)
    both_cube = jnp.concatenate([act_cube, grad_cube], axis=-1)
    flat_both = assemble_rows(relay(plan, both_cube, region_count), both_cube)
    forward, backward, weight_grad = convolve_flat(flat_both, BS, grad_out, conv_weight)
    block_output = (inputs + forward * mask_col).astype(jnp.bfloat16)
    slope = jax.nn.sigmoid(pre)
    dnorm = backward * mask_col * (slope * (1.0 + pre * (1.0 - slope))) * norm_gain
    dinput = rinv * (dnorm - normed * jnp.mean(dnorm * normed, axis=-1, keepdims=True))
    input_grad = (cotangent[0, 0].astype(jnp.float32) + dinput).astype(jnp.bfloat16)
    flat_grad = weight_grad.reshape(-1, width)
    share_rows = flat_grad.shape[0] // region_count
    limit = math.sqrt(flat_grad.shape[0] * width)
    sizes = [lax.axis_size(name) for name in REGION_AXES]
    staged = lax.psum_scatter(
        flat_grad.reshape(*sizes, share_rows, width), REGION_AXES[-1], scatter_dimension=2, tiled=True
    ).reshape(*sizes[:2], share_rows, width)
    staged = direct_scatter_sum(staged, REGION_AXES[1], 1)
    share = direct_scatter_sum(staged, REGION_AXES[0], 0)
    scene_count = lax.axis_size("scene")
    total_squares = direct_sum(jnp.sum(share * share), REGION_AXES)
    factor = jnp.minimum(1.0, limit / jnp.sqrt(total_squares))
    update = butterfly_sum(share * factor, ("scene",)) / scene_count
    return (block_output.reshape(features.shape), input_grad.reshape(cotangent.shape), update)


def solution(mesh):
    split = jax.sharding.Mesh(
        mesh.devices.reshape(mesh.shape["scene"], 8, 4, 2), ("scene",) + REGION_AXES
    )
    in_specs = (
        P("scene", REGION_AXES, None, None),
        P("scene", REGION_AXES, None),
        P("scene", REGION_AXES, None, None),
        P(),
        P(),
        P("scene", None),
    )
    out_specs = (
        P("scene", REGION_AXES, None, None),
        P("scene", REGION_AXES, None, None),
        P(REGION_AXES, None),
    )
    return jax.shard_map(body, mesh=split, in_specs=in_specs, out_specs=out_specs, check_vma=False)
```

```python
import math

import jax
import jax.numpy as jnp
import numpy as np
from jax import lax
from jax.sharding import PartitionSpec as P

BS = 12
TAPS = 27
GY = 4
GZ = 2


NORM_EPSILON = 1e-06
OFFSETS = [(a, b, c) for a in (-1, 0, 1) for b in (-1, 0, 1) for c in (-1, 0, 1)]
DIRECTIONS = [
    item
    for level in (1, 2, 3)
    for item in OFFSETS
    if abs(item[0]) + abs(item[1]) + abs(item[2]) == level
]
COLUMNS = [(a, b) for a in (-1, 0, 1) for b in (-1, 0, 1)]


def side_range(component, edge):
    if component == 1:
        return (edge - 1, edge)
    if component == -1:
        return (0, 1)
    return (0, edge)


def halo_range(component, edge):
    if component == 1:
        return (edge + 1, edge + 2)
    if component == -1:
        return (0, 1)
    return (1, edge + 1)


def slab_count(direction, edge):
    total = 1
    for component in direction:
        total = total * (1 if component != 0 else edge)
    return total


def row_directions(edge, region_count):
    labels = []
    for position, direction in enumerate(DIRECTIONS):
        labels = labels + [position] * slab_count(direction, edge)
    per_peer = -(-len(labels) // region_count)
    labels = labels + [len(DIRECTIONS)] * (per_peer * region_count - len(labels))
    return (np.array(labels, dtype=np.int32).reshape(per_peer, region_count), len(labels), per_peer)


def plan_sources(owner_row, labels_now, region_count):
    slot_ids = jnp.arange(region_count, dtype=jnp.int32)
    block_of = jnp.sum(
        jnp.where(owner_row[None, :] == slot_ids[:, None], slot_ids[None, :], 0), axis=1
    )
    layer = GY * GZ
    across = region_count // layer
    table = np.array(DIRECTIONS + [(0, 0, 0)], dtype=np.int32)
    real = np.arange(len(DIRECTIONS) + 1) < len(DIRECTIONS)
    pick = labels_now[:, None] == np.arange(len(DIRECTIONS) + 1, dtype=np.int32)[None, :]
    step = jnp.sum(jnp.where(pick[:, :, None], table[None, :, :], 0), axis=1)
    usable = jnp.any(pick & real[None, :], axis=1)
    near_x = (block_of // layer)[:, None] + step[None, :, 0]
    near_y = (block_of // GZ % GY)[:, None] + step[None, :, 1]
    near_z = (block_of % GZ)[:, None] + step[None, :, 2]
    inside = (
        usable[None, :]
        & (near_x >= 0)
        & (near_x < across)
        & (near_y >= 0)
        & (near_y < GY)
        & (near_z >= 0)
        & (near_z < GZ)
    )
    target = near_x * layer + near_y * GZ + near_z
    holder = jnp.sum(
        jnp.where(target[:, :, None] == slot_ids[None, None, :], owner_row[None, None, :], 0), axis=2
    )
    return jnp.where(inside, holder, -1)


def route_plan(owner_row, region_count):
    labels, padded_rows, per_peer = row_directions(BS, region_count)
    myself = lax.axis_index(REGION_AXES)
    labels_now = lax.dynamic_index_in_dim(jnp.asarray(labels), myself, 1, keepdims=False)
    sources = plan_sources(owner_row, labels_now, region_count)
    valid = sources >= 0
    positions = jnp.arange(per_peer, dtype=jnp.int32)[None, :]
    source_rows = jnp.where(valid, sources * per_peer + positions, 0).reshape(-1)
    return (source_rows, valid.astype(jnp.bfloat16), per_peer)


def pick_rows(holdings, plan):
    source_rows, valid, per_peer = plan
    width = holdings.shape[2]
    flat = holdings.reshape(-1, width)
    picked = jnp.take(flat, source_rows, axis=0).reshape(holdings.shape[0], per_peer, width)
    return picked * valid[..., None]


def shell_index(edge, region_count, per_peer):
    cube_ids = np.arange(edge * edge * edge).reshape(edge, edge, edge)
    pieces = []
    for direction in DIRECTIONS:
        spans = [side_range(-component, edge) for component in direction]
        pieces.append(
            cube_ids[
                spans[0][0] : spans[0][1], spans[1][0] : spans[1][1], spans[2][0] : spans[2][1]
            ].reshape(-1)
        )
    rows = np.concatenate(pieces)
    rows = np.pad(rows, (0, per_peer * region_count - rows.size))
    return rows.reshape(per_peer, region_count).T.reshape(-1).astype(np.int32)


def assemble_index(edge, region_count, per_peer):
    side = edge + 2
    inner = edge * edge * edge
    table = np.zeros((side, side, side), np.int64)
    table[1 : edge + 1, 1 : edge + 1, 1 : edge + 1] = np.arange(inner).reshape(edge, edge, edge)
    offset = 0
    for direction in DIRECTIONS:
        spans = [halo_range(component, edge) for component in direction]
        lengths = [upper - lower for lower, upper in spans]
        count = lengths[0] * lengths[1] * lengths[2]
        whole_rows = offset + np.arange(count)
        sources = inner + (whole_rows % region_count) * per_peer + whole_rows // region_count
        table[
            spans[0][0] : spans[0][1], spans[1][0] : spans[1][1], spans[2][0] : spans[2][1]
        ] = sources.reshape(lengths)
        offset = offset + count
    return table.reshape(-1).astype(np.int32)


def dealt_rows(cube, region_count, per_peer):
    width = cube.shape[3]
    index = shell_index(cube.shape[0], region_count, per_peer)
    picked = jnp.take(cube.reshape(-1, width), index, axis=0, mode="clip")
    return picked.reshape(region_count, per_peer, width)


def assemble_rows(received, cube):
    width = cube.shape[3]
    index = assemble_index(cube.shape[0], received.shape[0], received.shape[1])
    source = jnp.concatenate([cube.reshape(-1, width), received.reshape(-1, width)], axis=0)
    return jnp.take(source, index, axis=0, mode="clip")


def relay(plan, cube, region_count):
    dealt = lax.all_to_all(
        dealt_rows(cube, region_count, plan[2]), REGION_AXES, split_axis=0, concat_axis=0, tiled=True
    )
    return lax.all_to_all(pick_rows(dealt, plan), REGION_AXES, split_axis=0, concat_axis=0, tiled=True)


REGION_AXES = ("z", "y", "core")


def direct_scatter_sum(blocks, name, axis):
    size = lax.axis_size(name)
    me = lax.axis_index(name)
    total = lax.dynamic_index_in_dim(blocks, me, axis, keepdims=False)
    for shift in range(1, size):
        piece = lax.dynamic_index_in_dim(blocks, (me + shift) % size, axis, keepdims=False)
        pairs = [(index, (index + shift) % size) for index in range(size)]
        total = total + lax.ppermute(piece, name, pairs)
    return total


def direct_sum(value, names):
    for name in names:
        size = lax.axis_size(name)
        received = [
            lax.ppermute(value, name, [(index, (index + shift) % size) for index in range(size)])
            for shift in range(1, size)
        ]
        for piece in received:
            value = value + piece
    return value


def butterfly_sum(value, names):
    for name in names:
        size = lax.axis_size(name)
        stride = 1
        while stride < size:
            pairs = [(index, index ^ stride) for index in range(size)]
            value = value + lax.ppermute(value, name, pairs)
            stride = stride * 2
    return value


def convolve_flat(flat, edge, grad_block, conv_weight):
    side = edge + 2
    width = grad_block.shape[1]
    plane = side * side
    base = plane + side + 1
    span = (edge - 1) * plane + (edge - 1) * side + edge
    zero_row = jnp.zeros((1, 2 * width), flat.dtype)
    after = jnp.concatenate([flat[1:], zero_row], axis=0)
    before = jnp.concatenate([zero_row, flat[:-1]], axis=0)
    act_rows = jnp.concatenate([before[:, :width], flat[:, :width], after[:, :width]], axis=1)
    grad_rows = jnp.concatenate([after[:, width:], flat[:, width:], before[:, width:]], axis=1)
    own = jnp.pad(grad_block.reshape(edge, edge, edge, width), ((1, 1), (1, 1), (1, 1), (0, 0)))
    own = own.reshape(-1, width)[base : base + span]
    forward = jnp.zeros((span, width), jnp.float32)
    backward = jnp.zeros((span, width), jnp.float32)
    terms = []
    for group_index, (shift_x, shift_y) in enumerate(COLUMNS):
        group_weight = conv_weight[3 * group_index : 3 * group_index + 3]
        start = base + shift_x * plane + shift_y * side
        window = act_rows[start : start + span]
        forward = forward + jnp.dot(
            window, group_weight.reshape(3 * width, width), preferred_element_type=jnp.float32
        )
        mirror_start = base - shift_x * plane - shift_y * side
        mirror = grad_rows[mirror_start : mirror_start + span]
        backward = backward + jnp.dot(
            mirror,
            group_weight.transpose(0, 2, 1).reshape(3 * width, width),
            preferred_element_type=jnp.float32,
        )
        terms.append(
            lax.dot_general(window, own, (((0,), (0,)), ((), ())), preferred_element_type=jnp.float32)
        )

    def interior(rows):
        rows = jnp.pad(rows, ((0, edge * plane - span), (0, 0)))
        return rows.reshape(edge, side, side, width)[:, :edge, :edge].reshape(-1, width)

    return (interior(forward), interior(backward), jnp.concatenate(terms, axis=0).reshape(TAPS, width, width))


def body(features, voxel_mask, cotangent, norm_gain, conv_weight, block_owner):
    width = features.shape[-1]
    region_count = math.prod(lax.axis_size(name) for name in REGION_AXES)
    plan = route_plan(block_owner[0], region_count)
    inputs = features[0, 0].astype(jnp.float32)
    mask_col = voxel_mask[0, 0].astype(jnp.float32)[:, None]
    rinv = lax.rsqrt(jnp.mean(inputs * inputs, axis=-1, keepdims=True) + NORM_EPSILON)
    normed = inputs * rinv
    pre = normed * norm_gain
    activity = (jax.nn.silu(pre) * mask_col).astype(jnp.bfloat16)
    grad_out = cotangent[0, 0] * voxel_mask[0, 0].astype(jnp.bfloat16)[:, None]
    act_cube = activity.reshape(BS, BS, BS, width)
    grad_cube = grad_out.reshape(BS, BS, BS, width)
    both_cube = jnp.concatenate([act_cube, grad_cube], axis=-1)
    flat_both = assemble_rows(relay(plan, both_cube, region_count), both_cube)
    forward, backward, weight_grad = convolve_flat(flat_both, BS, grad_out, conv_weight)
    block_output = (inputs + forward * mask_col).astype(jnp.bfloat16)
    slope = jax.nn.sigmoid(pre)
    dnorm = backward * mask_col * (slope * (1.0 + pre * (1.0 - slope))) * norm_gain
    dinput = rinv * (dnorm - normed * jnp.mean(dnorm * normed, axis=-1, keepdims=True))
    input_grad = (cotangent[0, 0].astype(jnp.float32) + dinput).astype(jnp.bfloat16)
    flat_grad = weight_grad.reshape(-1, width)
    share_rows = flat_grad.shape[0] // region_count
    limit = math.sqrt(flat_grad.shape[0] * width)
    sizes = [lax.axis_size(name) for name in REGION_AXES]
    staged = lax.psum_scatter(
        flat_grad.reshape(*sizes, share_rows, width), REGION_AXES[-1], scatter_dimension=2, tiled=True
    ).reshape(*sizes[:2], share_rows, width)
    staged = direct_scatter_sum(staged, REGION_AXES[1], 1)
    share = direct_scatter_sum(staged, REGION_AXES[0], 0)
    scene_count = lax.axis_size("scene")
    total_squares = direct_sum(jnp.sum(share * share), REGION_AXES)
    factor = jnp.minimum(1.0, limit / jnp.sqrt(total_squares))
    update = butterfly_sum(share * factor, ("scene",)) / scene_count
    return (block_output.reshape(features.shape), input_grad.reshape(cotangent.shape), update)


def solution(mesh):
    split = jax.sharding.Mesh(
        mesh.devices.reshape(mesh.shape["scene"], 8, 4, 2), ("scene",) + REGION_AXES
    )
    in_specs = (
        P("scene", REGION_AXES, None, None),
        P("scene", REGION_AXES, None),
        P("scene", REGION_AXES, None, None),
        P(),
        P(),
        P("scene", None),
    )
    out_specs = (
        P("scene", REGION_AXES, None, None),
        P("scene", REGION_AXES, None, None),
        P(REGION_AXES, None),
    )
    return jax.shard_map(body, mesh=split, in_specs=in_specs, out_specs=out_specs, check_vma=False)
```

```python
import math

import jax
import jax.numpy as jnp
import numpy as np
from jax import lax
from jax.sharding import PartitionSpec as P

BS = 12
TAPS = 27
GY = 4
GZ = 2


NORM_EPSILON = 1e-06
OFFSETS = [(a, b, c) for a in (-1, 0, 1) for b in (-1, 0, 1) for c in (-1, 0, 1)]
DIRECTIONS = [
    item
    for level in (1, 2, 3)
    for item in OFFSETS
    if abs(item[0]) + abs(item[1]) + abs(item[2]) == level
]
COLUMNS = [(a, b) for a in (-1, 0, 1) for b in (-1, 0, 1)]


def side_range(component, edge):
    if component == 1:
        return (edge - 1, edge)
    if component == -1:
        return (0, 1)
    return (0, edge)


def halo_range(component, edge):
    if component == 1:
        return (edge + 1, edge + 2)
    if component == -1:
        return (0, 1)
    return (1, edge + 1)


def slab_count(direction, edge):
    total = 1
    for component in direction:
        total = total * (1 if component != 0 else edge)
    return total


def row_directions(edge, region_count):
    labels = []
    for position, direction in enumerate(DIRECTIONS):
        labels = labels + [position] * slab_count(direction, edge)
    per_peer = -(-len(labels) // region_count)
    labels = labels + [len(DIRECTIONS)] * (per_peer * region_count - len(labels))
    return (np.array(labels, dtype=np.int32).reshape(per_peer, region_count), len(labels), per_peer)


def plan_sources(owner_row, labels_now, region_count):
    slot_ids = jnp.arange(region_count, dtype=jnp.int32)
    block_of = jnp.sum(
        jnp.where(owner_row[None, :] == slot_ids[:, None], slot_ids[None, :], 0), axis=1
    )
    layer = GY * GZ
    across = region_count // layer
    table = np.array(DIRECTIONS + [(0, 0, 0)], dtype=np.int32)
    real = np.arange(len(DIRECTIONS) + 1) < len(DIRECTIONS)
    pick = labels_now[:, None] == np.arange(len(DIRECTIONS) + 1, dtype=np.int32)[None, :]
    step = jnp.sum(jnp.where(pick[:, :, None], table[None, :, :], 0), axis=1)
    usable = jnp.any(pick & real[None, :], axis=1)
    near_x = (block_of // layer)[:, None] + step[None, :, 0]
    near_y = (block_of // GZ % GY)[:, None] + step[None, :, 1]
    near_z = (block_of % GZ)[:, None] + step[None, :, 2]
    inside = (
        usable[None, :]
        & (near_x >= 0)
        & (near_x < across)
        & (near_y >= 0)
        & (near_y < GY)
        & (near_z >= 0)
        & (near_z < GZ)
    )
    target = near_x * layer + near_y * GZ + near_z
    holder = jnp.sum(
        jnp.where(target[:, :, None] == slot_ids[None, None, :], owner_row[None, None, :], 0), axis=2
    )
    return jnp.where(inside, holder, -1)


def route_plan(owner_row, region_count):
    labels, padded_rows, per_peer = row_directions(BS, region_count)
    myself = lax.axis_index(REGION_AXES)
    labels_now = lax.dynamic_index_in_dim(jnp.asarray(labels), myself, 1, keepdims=False)
    sources = plan_sources(owner_row, labels_now, region_count)
    valid = sources >= 0
    positions = jnp.arange(per_peer, dtype=jnp.int32)[None, :]
    source_rows = jnp.where(valid, sources * per_peer + positions, 0).reshape(-1)
    return (source_rows, valid.astype(jnp.bfloat16), per_peer)


def pick_rows(holdings, plan):
    source_rows, valid, per_peer = plan
    width = holdings.shape[2]
    flat = holdings.reshape(-1, width)
    picked = jnp.take(flat, source_rows, axis=0).reshape(holdings.shape[0], per_peer, width)
    return picked * valid[..., None]


def shell_index(edge, region_count, per_peer):
    cube_ids = np.arange(edge * edge * edge).reshape(edge, edge, edge)
    pieces = []
    for direction in DIRECTIONS:
        spans = [side_range(-component, edge) for component in direction]
        pieces.append(
            cube_ids[
                spans[0][0] : spans[0][1], spans[1][0] : spans[1][1], spans[2][0] : spans[2][1]
            ].reshape(-1)
        )
    rows = np.concatenate(pieces)
    rows = np.pad(rows, (0, per_peer * region_count - rows.size))
    return rows.reshape(per_peer, region_count).T.reshape(-1).astype(np.int32)


def assemble_index(edge, region_count, per_peer):
    side = edge + 2
    inner = edge * edge * edge
    table = np.zeros((side, side, side), np.int64)
    table[1 : edge + 1, 1 : edge + 1, 1 : edge + 1] = np.arange(inner).reshape(edge, edge, edge)
    offset = 0
    for direction in DIRECTIONS:
        spans = [halo_range(component, edge) for component in direction]
        lengths = [upper - lower for lower, upper in spans]
        count = lengths[0] * lengths[1] * lengths[2]
        whole_rows = offset + np.arange(count)
        sources = inner + (whole_rows % region_count) * per_peer + whole_rows // region_count
        table[
            spans[0][0] : spans[0][1], spans[1][0] : spans[1][1], spans[2][0] : spans[2][1]
        ] = sources.reshape(lengths)
        offset = offset + count
    return table.reshape(-1).astype(np.int32)


def dealt_rows(cube, region_count, per_peer):
    width = cube.shape[3]
    index = shell_index(cube.shape[0], region_count, per_peer)
    picked = jnp.take(cube.reshape(-1, width), index, axis=0, mode="clip")
    return picked.reshape(region_count, per_peer, width)


def assemble_rows(received, cube):
    width = cube.shape[3]
    index = assemble_index(cube.shape[0], received.shape[0], received.shape[1])
    source = jnp.concatenate([cube.reshape(-1, width), received.reshape(-1, width)], axis=0)
    return jnp.take(source, index, axis=0, mode="clip")


def relay(plan, cube, region_count):
    dealt = lax.all_to_all(
        dealt_rows(cube, region_count, plan[2]), REGION_AXES, split_axis=0, concat_axis=0, tiled=True
    )
    return lax.all_to_all(pick_rows(dealt, plan), REGION_AXES, split_axis=0, concat_axis=0, tiled=True)


REGION_AXES = ("z", "y", "core")


def direct_scatter_sum(blocks, name, axis):
    size = lax.axis_size(name)
    me = lax.axis_index(name)
    total = lax.dynamic_index_in_dim(blocks, me, axis, keepdims=False)
    for shift in range(1, size):
        piece = lax.dynamic_index_in_dim(blocks, (me + shift) % size, axis, keepdims=False)
        pairs = [(index, (index + shift) % size) for index in range(size)]
        total = total + lax.ppermute(piece, name, pairs)
    return total


def direct_sum(value, names):
    for name in names:
        size = lax.axis_size(name)
        received = [
            lax.ppermute(value, name, [(index, (index + shift) % size) for index in range(size)])
            for shift in range(1, size)
        ]
        for piece in received:
            value = value + piece
    return value


def spread_sum(value, names):
    count = math.prod(lax.axis_size(name) for name in names)
    copies = jnp.broadcast_to(value[None], (count,) + value.shape)
    received = lax.all_to_all(copies, names, split_axis=0, concat_axis=0, tiled=True)
    total = received[0]
    for index in range(1, count):
        total = total + received[index]
    return total


def butterfly_sum(value, names):
    for name in names:
        size = lax.axis_size(name)
        stride = 1
        while stride < size:
            pairs = [(index, index ^ stride) for index in range(size)]
            value = value + lax.ppermute(value, name, pairs)
            stride = stride * 2
    return value


def convolve_flat(flat, edge, grad_block, conv_weight):
    side = edge + 2
    width = grad_block.shape[1]
    plane = side * side
    base = plane + side + 1
    span = (edge - 1) * plane + (edge - 1) * side + edge
    zero_row = jnp.zeros((1, 2 * width), flat.dtype)
    after = jnp.concatenate([flat[1:], zero_row], axis=0)
    before = jnp.concatenate([zero_row, flat[:-1]], axis=0)
    act_rows = jnp.concatenate([before[:, :width], flat[:, :width], after[:, :width]], axis=1)
    grad_rows = jnp.concatenate([after[:, width:], flat[:, width:], before[:, width:]], axis=1)
    own = jnp.pad(grad_block.reshape(edge, edge, edge, width), ((1, 1), (1, 1), (1, 1), (0, 0)))
    own = own.reshape(-1, width)[base : base + span]
    forward = jnp.zeros((span, width), jnp.float32)
    backward = jnp.zeros((span, width), jnp.float32)
    terms = []
    for group_index, (shift_x, shift_y) in enumerate(COLUMNS):
        group_weight = conv_weight[3 * group_index : 3 * group_index + 3]
        start = base + shift_x * plane + shift_y * side
        window = act_rows[start : start + span]
        forward = forward + jnp.dot(
            window, group_weight.reshape(3 * width, width), preferred_element_type=jnp.float32
        )
        mirror_start = base - shift_x * plane - shift_y * side
        mirror = grad_rows[mirror_start : mirror_start + span]
        backward = backward + jnp.dot(
            mirror,
            group_weight.transpose(0, 2, 1).reshape(3 * width, width),
            preferred_element_type=jnp.float32,
        )
        terms.append(
            lax.dot_general(window, own, (((0,), (0,)), ((), ())), preferred_element_type=jnp.float32)
        )

    def interior(rows):
        rows = jnp.pad(rows, ((0, edge * plane - span), (0, 0)))
        return rows.reshape(edge, side, side, width)[:, :edge, :edge].reshape(-1, width)

    return (interior(forward), interior(backward), jnp.concatenate(terms, axis=0).reshape(TAPS, width, width))


def body(features, voxel_mask, cotangent, norm_gain, conv_weight, block_owner):
    width = features.shape[-1]
    region_count = math.prod(lax.axis_size(name) for name in REGION_AXES)
    plan = route_plan(block_owner[0], region_count)
    inputs = features[0, 0].astype(jnp.float32)
    mask_col = voxel_mask[0, 0].astype(jnp.float32)[:, None]
    rinv = lax.rsqrt(jnp.mean(inputs * inputs, axis=-1, keepdims=True) + NORM_EPSILON)
    normed = inputs * rinv
    pre = normed * norm_gain
    activity = (jax.nn.silu(pre) * mask_col).astype(jnp.bfloat16)
    grad_out = cotangent[0, 0] * voxel_mask[0, 0].astype(jnp.bfloat16)[:, None]
    act_cube = activity.reshape(BS, BS, BS, width)
    grad_cube = grad_out.reshape(BS, BS, BS, width)
    both_cube = jnp.concatenate([act_cube, grad_cube], axis=-1)
    flat_both = assemble_rows(relay(plan, both_cube, region_count), both_cube)
    forward, backward, weight_grad = convolve_flat(flat_both, BS, grad_out, conv_weight)
    block_output = (inputs + forward * mask_col).astype(jnp.bfloat16)
    slope = jax.nn.sigmoid(pre)
    dnorm = backward * mask_col * (slope * (1.0 + pre * (1.0 - slope))) * norm_gain
    dinput = rinv * (dnorm - normed * jnp.mean(dnorm * normed, axis=-1, keepdims=True))
    input_grad = (cotangent[0, 0].astype(jnp.float32) + dinput).astype(jnp.bfloat16)
    flat_grad = weight_grad.reshape(-1, width)
    share_rows = flat_grad.shape[0] // region_count
    limit = math.sqrt(flat_grad.shape[0] * width)
    sizes = [lax.axis_size(name) for name in REGION_AXES]
    staged = lax.psum_scatter(
        flat_grad.reshape(*sizes, share_rows, width), REGION_AXES[-1], scatter_dimension=2, tiled=True
    ).reshape(*sizes[:2], share_rows, width)
    staged = direct_scatter_sum(staged, REGION_AXES[1], 1)
    share = direct_scatter_sum(staged, REGION_AXES[0], 0)
    scene_count = lax.axis_size("scene")
    total_squares = spread_sum(jnp.broadcast_to(jnp.sum(share * share), (8, width)), REGION_AXES)[0, 0]
    factor = jnp.minimum(1.0, limit / jnp.sqrt(total_squares))
    update = spread_sum(share * factor, ("scene",)) / scene_count
    return (block_output.reshape(features.shape), input_grad.reshape(cotangent.shape), update)


def solution(mesh):
    split = jax.sharding.Mesh(
        mesh.devices.reshape(mesh.shape["scene"], 8, 4, 2), ("scene",) + REGION_AXES
    )
    in_specs = (
        P("scene", REGION_AXES, None, None),
        P("scene", REGION_AXES, None),
        P("scene", REGION_AXES, None, None),
        P(),
        P(),
        P("scene", None),
    )
    out_specs = (
        P("scene", REGION_AXES, None, None),
        P("scene", REGION_AXES, None, None),
        P(REGION_AXES, None),
    )
    return jax.shard_map(body, mesh=split, in_specs=in_specs, out_specs=out_specs, check_vma=False)
```

```python
import math

import jax
import jax.numpy as jnp
import numpy as np
from jax import lax
from jax.sharding import PartitionSpec as P

BS = 12
TAPS = 27
GY = 4
GZ = 2


NORM_EPSILON = 1e-06
OFFSETS = [(a, b, c) for a in (-1, 0, 1) for b in (-1, 0, 1) for c in (-1, 0, 1)]
DIRECTIONS = [
    item
    for level in (1, 2, 3)
    for item in OFFSETS
    if abs(item[0]) + abs(item[1]) + abs(item[2]) == level
]
COLUMNS = [(a, b) for a in (-1, 0, 1) for b in (-1, 0, 1)]


def side_range(component, edge):
    if component == 1:
        return (edge - 1, edge)
    if component == -1:
        return (0, 1)
    return (0, edge)


def halo_range(component, edge):
    if component == 1:
        return (edge + 1, edge + 2)
    if component == -1:
        return (0, 1)
    return (1, edge + 1)


def slab_count(direction, edge):
    total = 1
    for component in direction:
        total = total * (1 if component != 0 else edge)
    return total


def row_directions(edge, region_count):
    labels = []
    for position, direction in enumerate(DIRECTIONS):
        labels = labels + [position] * slab_count(direction, edge)
    per_peer = -(-len(labels) // region_count)
    labels = labels + [len(DIRECTIONS)] * (per_peer * region_count - len(labels))
    return (np.array(labels, dtype=np.int32).reshape(per_peer, region_count), len(labels), per_peer)


def plan_sources(owner_row, labels_now, region_count):
    slot_ids = jnp.arange(region_count, dtype=jnp.int32)
    block_of = jnp.sum(
        jnp.where(owner_row[None, :] == slot_ids[:, None], slot_ids[None, :], 0), axis=1
    )
    layer = GY * GZ
    across = region_count // layer
    table = np.array(DIRECTIONS + [(0, 0, 0)], dtype=np.int32)
    real = np.arange(len(DIRECTIONS) + 1) < len(DIRECTIONS)
    pick = labels_now[:, None] == np.arange(len(DIRECTIONS) + 1, dtype=np.int32)[None, :]
    step = jnp.sum(jnp.where(pick[:, :, None], table[None, :, :], 0), axis=1)
    usable = jnp.any(pick & real[None, :], axis=1)
    near_x = (block_of // layer)[:, None] + step[None, :, 0]
    near_y = (block_of // GZ % GY)[:, None] + step[None, :, 1]
    near_z = (block_of % GZ)[:, None] + step[None, :, 2]
    inside = (
        usable[None, :]
        & (near_x >= 0)
        & (near_x < across)
        & (near_y >= 0)
        & (near_y < GY)
        & (near_z >= 0)
        & (near_z < GZ)
    )
    target = near_x * layer + near_y * GZ + near_z
    holder = jnp.sum(
        jnp.where(target[:, :, None] == slot_ids[None, None, :], owner_row[None, None, :], 0), axis=2
    )
    return jnp.where(inside, holder, -1)


def route_plan(owner_row, region_count):
    labels, padded_rows, per_peer = row_directions(BS, region_count)
    myself = lax.axis_index(REGION_AXES)
    labels_now = lax.dynamic_index_in_dim(jnp.asarray(labels), myself, 1, keepdims=False)
    sources = plan_sources(owner_row, labels_now, region_count)
    valid = sources >= 0
    positions = jnp.arange(per_peer, dtype=jnp.int32)[None, :]
    source_rows = jnp.where(valid, sources * per_peer + positions, 0).reshape(-1)
    return (source_rows, valid.astype(jnp.bfloat16), per_peer)


def pick_rows(holdings, plan):
    source_rows, valid, per_peer = plan
    width = holdings.shape[2]
    flat = holdings.reshape(-1, width)
    picked = jnp.take(flat, source_rows, axis=0).reshape(holdings.shape[0], per_peer, width)
    return picked * valid[..., None]


def shell_index(edge, region_count, per_peer):
    cube_ids = np.arange(edge * edge * edge).reshape(edge, edge, edge)
    pieces = []
    for direction in DIRECTIONS:
        spans = [side_range(-component, edge) for component in direction]
        pieces.append(
            cube_ids[
                spans[0][0] : spans[0][1], spans[1][0] : spans[1][1], spans[2][0] : spans[2][1]
            ].reshape(-1)
        )
    rows = np.concatenate(pieces)
    rows = np.pad(rows, (0, per_peer * region_count - rows.size))
    return rows.reshape(per_peer, region_count).T.reshape(-1).astype(np.int32)


def assemble_index(edge, region_count, per_peer):
    side = edge + 2
    inner = edge * edge * edge
    table = np.zeros((side, side, side), np.int64)
    table[1 : edge + 1, 1 : edge + 1, 1 : edge + 1] = np.arange(inner).reshape(edge, edge, edge)
    offset = 0
    for direction in DIRECTIONS:
        spans = [halo_range(component, edge) for component in direction]
        lengths = [upper - lower for lower, upper in spans]
        count = lengths[0] * lengths[1] * lengths[2]
        whole_rows = offset + np.arange(count)
        sources = inner + (whole_rows % region_count) * per_peer + whole_rows // region_count
        table[
            spans[0][0] : spans[0][1], spans[1][0] : spans[1][1], spans[2][0] : spans[2][1]
        ] = sources.reshape(lengths)
        offset = offset + count
    return table.reshape(-1).astype(np.int32)


def dealt_rows(cube, region_count, per_peer):
    width = cube.shape[3]
    index = shell_index(cube.shape[0], region_count, per_peer)
    picked = jnp.take(cube.reshape(-1, width), index, axis=0, mode="clip")
    return picked.reshape(region_count, per_peer, width)


def assemble_rows(received, cube):
    width = cube.shape[3]
    index = assemble_index(cube.shape[0], received.shape[0], received.shape[1])
    source = jnp.concatenate([cube.reshape(-1, width), received.reshape(-1, width)], axis=0)
    return jnp.take(source, index, axis=0, mode="clip")


def relay(plan, cube, region_count):
    dealt = lax.all_to_all(
        dealt_rows(cube, region_count, plan[2]), REGION_AXES, split_axis=0, concat_axis=0, tiled=True
    )
    return lax.all_to_all(pick_rows(dealt, plan), REGION_AXES, split_axis=0, concat_axis=0, tiled=True)


REGION_AXES = ("z", "y", "core")


def direct_scatter_sum(blocks, name, axis):
    size = lax.axis_size(name)
    me = lax.axis_index(name)
    total = lax.dynamic_index_in_dim(blocks, me, axis, keepdims=False)
    for shift in range(1, size):
        piece = lax.dynamic_index_in_dim(blocks, (me + shift) % size, axis, keepdims=False)
        pairs = [(index, (index + shift) % size) for index in range(size)]
        total = total + lax.ppermute(piece, name, pairs)
    return total


def direct_sum(value, names):
    for name in names:
        size = lax.axis_size(name)
        received = [
            lax.ppermute(value, name, [(index, (index + shift) % size) for index in range(size)])
            for shift in range(1, size)
        ]
        for piece in received:
            value = value + piece
    return value


def exchange_sum(blocks, name, axis):
    received = lax.all_to_all(blocks, name, split_axis=axis, concat_axis=axis, tiled=True)
    pieces = [lax.index_in_dim(received, index, axis, keepdims=False) for index in range(blocks.shape[axis])]
    total = pieces[0]
    for piece in pieces[1:]:
        total = total + piece
    return total


def spread_sum(value, names):
    count = math.prod(lax.axis_size(name) for name in names)
    copies = jnp.broadcast_to(value[None], (count,) + value.shape)
    received = lax.all_to_all(copies, names, split_axis=0, concat_axis=0, tiled=True)
    total = received[0]
    for index in range(1, count):
        total = total + received[index]
    return total


def butterfly_sum(value, names):
    for name in names:
        size = lax.axis_size(name)
        stride = 1
        while stride < size:
            pairs = [(index, index ^ stride) for index in range(size)]
            value = value + lax.ppermute(value, name, pairs)
            stride = stride * 2
    return value


def convolve_flat(flat, edge, grad_block, conv_weight):
    side = edge + 2
    width = grad_block.shape[1]
    plane = side * side
    base = plane + side + 1
    span = (edge - 1) * plane + (edge - 1) * side + edge
    zero_row = jnp.zeros((1, 2 * width), flat.dtype)
    after = jnp.concatenate([flat[1:], zero_row], axis=0)
    before = jnp.concatenate([zero_row, flat[:-1]], axis=0)
    act_rows = jnp.concatenate([before[:, :width], flat[:, :width], after[:, :width]], axis=1)
    grad_rows = jnp.concatenate([after[:, width:], flat[:, width:], before[:, width:]], axis=1)
    own = jnp.pad(grad_block.reshape(edge, edge, edge, width), ((1, 1), (1, 1), (1, 1), (0, 0)))
    own = own.reshape(-1, width)[base : base + span]
    forward = jnp.zeros((span, width), jnp.float32)
    backward = jnp.zeros((span, width), jnp.float32)
    terms = []
    for group_index, (shift_x, shift_y) in enumerate(COLUMNS):
        group_weight = conv_weight[3 * group_index : 3 * group_index + 3]
        start = base + shift_x * plane + shift_y * side
        window = act_rows[start : start + span]
        forward = forward + jnp.dot(
            window, group_weight.reshape(3 * width, width), preferred_element_type=jnp.float32
        )
        mirror_start = base - shift_x * plane - shift_y * side
        mirror = grad_rows[mirror_start : mirror_start + span]
        backward = backward + jnp.dot(
            mirror,
            group_weight.transpose(0, 2, 1).reshape(3 * width, width),
            preferred_element_type=jnp.float32,
        )
        terms.append(
            lax.dot_general(window, own, (((0,), (0,)), ((), ())), preferred_element_type=jnp.float32)
        )

    def interior(rows):
        rows = jnp.pad(rows, ((0, edge * plane - span), (0, 0)))
        return rows.reshape(edge, side, side, width)[:, :edge, :edge].reshape(-1, width)

    return (interior(forward), interior(backward), jnp.concatenate(terms, axis=0).reshape(TAPS, width, width))


def body(features, voxel_mask, cotangent, norm_gain, conv_weight, block_owner):
    width = features.shape[-1]
    region_count = math.prod(lax.axis_size(name) for name in REGION_AXES)
    plan = route_plan(block_owner[0], region_count)
    inputs = features[0, 0].astype(jnp.float32)
    mask_col = voxel_mask[0, 0].astype(jnp.float32)[:, None]
    rinv = lax.rsqrt(jnp.mean(inputs * inputs, axis=-1, keepdims=True) + NORM_EPSILON)
    normed = inputs * rinv
    pre = normed * norm_gain
    activity = (jax.nn.silu(pre) * mask_col).astype(jnp.bfloat16)
    grad_out = cotangent[0, 0] * voxel_mask[0, 0].astype(jnp.bfloat16)[:, None]
    act_cube = activity.reshape(BS, BS, BS, width)
    grad_cube = grad_out.reshape(BS, BS, BS, width)
    both_cube = jnp.concatenate([act_cube, grad_cube], axis=-1)
    flat_both = assemble_rows(relay(plan, both_cube, region_count), both_cube)
    forward, backward, weight_grad = convolve_flat(flat_both, BS, grad_out, conv_weight)
    block_output = (inputs + forward * mask_col).astype(jnp.bfloat16)
    slope = jax.nn.sigmoid(pre)
    dnorm = backward * mask_col * (slope * (1.0 + pre * (1.0 - slope))) * norm_gain
    dinput = rinv * (dnorm - normed * jnp.mean(dnorm * normed, axis=-1, keepdims=True))
    input_grad = (cotangent[0, 0].astype(jnp.float32) + dinput).astype(jnp.bfloat16)
    flat_grad = weight_grad.reshape(-1, width)
    share_rows = flat_grad.shape[0] // region_count
    limit = math.sqrt(flat_grad.shape[0] * width)
    sizes = [lax.axis_size(name) for name in REGION_AXES]
    staged = lax.psum_scatter(
        flat_grad.reshape(*sizes, share_rows, width), REGION_AXES[-1], scatter_dimension=2, tiled=True
    ).reshape(*sizes[:2], share_rows, width)
    staged = exchange_sum(staged, REGION_AXES[1], 1)
    share = exchange_sum(staged, REGION_AXES[0], 0)
    scene_count = lax.axis_size("scene")
    total_squares = spread_sum(jnp.broadcast_to(jnp.sum(share * share), (8, width)), REGION_AXES)[0, 0]
    factor = jnp.minimum(1.0, limit / jnp.sqrt(total_squares))
    update = spread_sum(share * factor, ("scene",)) / scene_count
    return (block_output.reshape(features.shape), input_grad.reshape(cotangent.shape), update)


def solution(mesh):
    split = jax.sharding.Mesh(
        mesh.devices.reshape(mesh.shape["scene"], 8, 4, 2), ("scene",) + REGION_AXES
    )
    in_specs = (
        P("scene", REGION_AXES, None, None),
        P("scene", REGION_AXES, None),
        P("scene", REGION_AXES, None, None),
        P(),
        P(),
        P("scene", None),
    )
    out_specs = (
        P("scene", REGION_AXES, None, None),
        P("scene", REGION_AXES, None, None),
        P(REGION_AXES, None),
    )
    return jax.shard_map(body, mesh=split, in_specs=in_specs, out_specs=out_specs, check_vma=False)
```

```python
import math

import jax
import jax.numpy as jnp
import numpy as np
from jax import lax
from jax.sharding import PartitionSpec as P

BS = 12
TAPS = 27
GY = 4
GZ = 2


NORM_EPSILON = 1e-06
OFFSETS = [(a, b, c) for a in (-1, 0, 1) for b in (-1, 0, 1) for c in (-1, 0, 1)]
DIRECTIONS = [
    item
    for level in (1, 2, 3)
    for item in OFFSETS
    if abs(item[0]) + abs(item[1]) + abs(item[2]) == level
]
COLUMNS = [(a, b) for a in (-1, 0, 1) for b in (-1, 0, 1)]


def side_range(component, edge):
    if component == 1:
        return (edge - 1, edge)
    if component == -1:
        return (0, 1)
    return (0, edge)


def halo_range(component, edge):
    if component == 1:
        return (edge + 1, edge + 2)
    if component == -1:
        return (0, 1)
    return (1, edge + 1)


def slab_count(direction, edge):
    total = 1
    for component in direction:
        total = total * (1 if component != 0 else edge)
    return total


def row_directions(edge, region_count):
    labels = []
    for position, direction in enumerate(DIRECTIONS):
        labels = labels + [position] * slab_count(direction, edge)
    per_peer = -(-len(labels) // region_count)
    labels = labels + [len(DIRECTIONS)] * (per_peer * region_count - len(labels))
    return (np.array(labels, dtype=np.int32).reshape(per_peer, region_count), len(labels), per_peer)


def plan_sources(owner_row, labels_now, region_count):
    slot_ids = jnp.arange(region_count, dtype=jnp.int32)
    block_of = jnp.sum(
        jnp.where(owner_row[None, :] == slot_ids[:, None], slot_ids[None, :], 0), axis=1
    )
    layer = GY * GZ
    across = region_count // layer
    table = np.array(DIRECTIONS + [(0, 0, 0)], dtype=np.int32)
    real = np.arange(len(DIRECTIONS) + 1) < len(DIRECTIONS)
    pick = labels_now[:, None] == np.arange(len(DIRECTIONS) + 1, dtype=np.int32)[None, :]
    step = jnp.sum(jnp.where(pick[:, :, None], table[None, :, :], 0), axis=1)
    usable = jnp.any(pick & real[None, :], axis=1)
    near_x = (block_of // layer)[:, None] + step[None, :, 0]
    near_y = (block_of // GZ % GY)[:, None] + step[None, :, 1]
    near_z = (block_of % GZ)[:, None] + step[None, :, 2]
    inside = (
        usable[None, :]
        & (near_x >= 0)
        & (near_x < across)
        & (near_y >= 0)
        & (near_y < GY)
        & (near_z >= 0)
        & (near_z < GZ)
    )
    target = near_x * layer + near_y * GZ + near_z
    holder = jnp.sum(
        jnp.where(target[:, :, None] == slot_ids[None, None, :], owner_row[None, None, :], 0), axis=2
    )
    return jnp.where(inside, holder, -1)


def route_plan(owner_row, region_count):
    labels, padded_rows, per_peer = row_directions(BS, region_count)
    myself = lax.axis_index(REGION_AXES)
    labels_now = lax.dynamic_index_in_dim(jnp.asarray(labels), myself, 1, keepdims=False)
    sources = plan_sources(owner_row, labels_now, region_count)
    valid = sources >= 0
    positions = jnp.arange(per_peer, dtype=jnp.int32)[None, :]
    source_rows = jnp.where(valid, sources * per_peer + positions, 0).reshape(-1)
    return (source_rows, valid.astype(jnp.bfloat16), per_peer)


def pick_rows(holdings, plan):
    source_rows, valid, per_peer = plan
    width = holdings.shape[2]
    flat = holdings.reshape(-1, width)
    picked = jnp.take(flat, source_rows, axis=0).reshape(holdings.shape[0], per_peer, width)
    return picked * valid[..., None]


def shell_index(edge, region_count, per_peer):
    cube_ids = np.arange(edge * edge * edge).reshape(edge, edge, edge)
    pieces = []
    for direction in DIRECTIONS:
        spans = [side_range(-component, edge) for component in direction]
        pieces.append(
            cube_ids[
                spans[0][0] : spans[0][1], spans[1][0] : spans[1][1], spans[2][0] : spans[2][1]
            ].reshape(-1)
        )
    rows = np.concatenate(pieces)
    rows = np.pad(rows, (0, per_peer * region_count - rows.size))
    return rows.reshape(per_peer, region_count).T.reshape(-1).astype(np.int32)


def assemble_index(edge, region_count, per_peer):
    side = edge + 2
    inner = edge * edge * edge
    table = np.zeros((side, side, side), np.int64)
    table[1 : edge + 1, 1 : edge + 1, 1 : edge + 1] = np.arange(inner).reshape(edge, edge, edge)
    offset = 0
    for direction in DIRECTIONS:
        spans = [halo_range(component, edge) for component in direction]
        lengths = [upper - lower for lower, upper in spans]
        count = lengths[0] * lengths[1] * lengths[2]
        whole_rows = offset + np.arange(count)
        sources = inner + (whole_rows % region_count) * per_peer + whole_rows // region_count
        table[
            spans[0][0] : spans[0][1], spans[1][0] : spans[1][1], spans[2][0] : spans[2][1]
        ] = sources.reshape(lengths)
        offset = offset + count
    return table.reshape(-1).astype(np.int32)


def dealt_rows(cube, region_count, per_peer):
    width = cube.shape[3]
    index = shell_index(cube.shape[0], region_count, per_peer)
    picked = jnp.take(cube.reshape(-1, width), index, axis=0, mode="clip")
    return picked.reshape(region_count, per_peer, width)


def assemble_rows(received, cube):
    width = cube.shape[3]
    index = assemble_index(cube.shape[0], received.shape[0], received.shape[1])
    source = jnp.concatenate([cube.reshape(-1, width), received.reshape(-1, width)], axis=0)
    return jnp.take(source, index, axis=0, mode="clip")


def relay(plan, cube, region_count):
    dealt = lax.all_to_all(
        dealt_rows(cube, region_count, plan[2]), REGION_AXES, split_axis=0, concat_axis=0, tiled=True
    )
    return lax.all_to_all(pick_rows(dealt, plan), REGION_AXES, split_axis=0, concat_axis=0, tiled=True)


REGION_AXES = ("z", "y", "core")


def direct_scatter_sum(blocks, name, axis):
    size = lax.axis_size(name)
    me = lax.axis_index(name)
    total = lax.dynamic_index_in_dim(blocks, me, axis, keepdims=False)
    for shift in range(1, size):
        piece = lax.dynamic_index_in_dim(blocks, (me + shift) % size, axis, keepdims=False)
        pairs = [(index, (index + shift) % size) for index in range(size)]
        total = total + lax.ppermute(piece, name, pairs)
    return total


def direct_sum(value, names):
    for name in names:
        size = lax.axis_size(name)
        received = [
            lax.ppermute(value, name, [(index, (index + shift) % size) for index in range(size)])
            for shift in range(1, size)
        ]
        for piece in received:
            value = value + piece
    return value


def exchange_sum(blocks, name, axis):
    received = lax.all_to_all(blocks, name, split_axis=axis, concat_axis=axis, tiled=True)
    pieces = [lax.index_in_dim(received, index, axis, keepdims=False) for index in range(blocks.shape[axis])]
    total = pieces[0]
    for piece in pieces[1:]:
        total = total + piece
    return total


def spread_sum(value, names):
    count = math.prod(lax.axis_size(name) for name in names)
    copies = jnp.broadcast_to(value[None], (count,) + value.shape)
    received = lax.all_to_all(copies, names, split_axis=0, concat_axis=0, tiled=True)
    total = received[0]
    for index in range(1, count):
        total = total + received[index]
    return total


def butterfly_sum(value, names):
    for name in names:
        size = lax.axis_size(name)
        stride = 1
        while stride < size:
            pairs = [(index, index ^ stride) for index in range(size)]
            value = value + lax.ppermute(value, name, pairs)
            stride = stride * 2
    return value


def convolve_flat(flat, edge, grad_block, conv_weight):
    side = edge + 2
    width = grad_block.shape[1]
    plane = side * side
    base = plane + side + 1
    span = (edge - 1) * plane + (edge - 1) * side + edge
    zero_row = jnp.zeros((1, 2 * width), flat.dtype)
    after = jnp.concatenate([flat[1:], zero_row], axis=0)
    before = jnp.concatenate([zero_row, flat[:-1]], axis=0)
    act_rows = jnp.concatenate([before[:, :width], flat[:, :width], after[:, :width]], axis=1)
    grad_rows = jnp.concatenate([after[:, width:], flat[:, width:], before[:, width:]], axis=1)
    own = jnp.pad(grad_block.reshape(edge, edge, edge, width), ((1, 1), (1, 1), (1, 1), (0, 0)))
    own = own.reshape(-1, width)[base : base + span]
    forward = jnp.zeros((span, width), jnp.float32)
    backward = jnp.zeros((span, width), jnp.float32)
    terms = []
    for group_index, (shift_x, shift_y) in enumerate(COLUMNS):
        group_weight = conv_weight[3 * group_index : 3 * group_index + 3]
        start = base + shift_x * plane + shift_y * side
        window = act_rows[start : start + span]
        forward = forward + jnp.dot(
            window, group_weight.reshape(3 * width, width), preferred_element_type=jnp.float32
        )
        mirror_start = base - shift_x * plane - shift_y * side
        mirror = grad_rows[mirror_start : mirror_start + span]
        backward = backward + jnp.dot(
            mirror,
            group_weight.transpose(0, 2, 1).reshape(3 * width, width),
            preferred_element_type=jnp.float32,
        )
        terms.append(
            lax.dot_general(window, own, (((0,), (0,)), ((), ())), preferred_element_type=jnp.float32)
        )

    def interior(rows):
        rows = jnp.pad(rows, ((0, edge * plane - span), (0, 0)))
        return rows.reshape(edge, side, side, width)[:, :edge, :edge].reshape(-1, width)

    return (interior(forward), interior(backward), jnp.concatenate(terms, axis=0).reshape(TAPS, width, width))


def body(features, voxel_mask, cotangent, norm_gain, conv_weight, block_owner):
    width = features.shape[-1]
    region_count = math.prod(lax.axis_size(name) for name in REGION_AXES)
    plan = route_plan(block_owner[0], region_count)
    inputs = features[0, 0].astype(jnp.float32)
    mask_col = voxel_mask[0, 0].astype(jnp.float32)[:, None]
    rinv = lax.rsqrt(jnp.mean(inputs * inputs, axis=-1, keepdims=True) + NORM_EPSILON)
    normed = inputs * rinv
    pre = normed * norm_gain
    activity = (jax.nn.silu(pre) * mask_col).astype(jnp.bfloat16)
    grad_out = cotangent[0, 0] * voxel_mask[0, 0].astype(jnp.bfloat16)[:, None]
    act_cube = activity.reshape(BS, BS, BS, width)
    grad_cube = grad_out.reshape(BS, BS, BS, width)
    both_cube = jnp.concatenate([act_cube, grad_cube], axis=-1)
    flat_both = assemble_rows(relay(plan, both_cube, region_count), both_cube)
    forward, backward, weight_grad = convolve_flat(flat_both, BS, grad_out, conv_weight)
    block_output = (inputs + forward * mask_col).astype(jnp.bfloat16)
    slope = jax.nn.sigmoid(pre)
    dnorm = backward * mask_col * (slope * (1.0 + pre * (1.0 - slope))) * norm_gain
    dinput = rinv * (dnorm - normed * jnp.mean(dnorm * normed, axis=-1, keepdims=True))
    input_grad = (cotangent[0, 0].astype(jnp.float32) + dinput).astype(jnp.bfloat16)
    flat_grad = weight_grad.reshape(-1, width)
    share_rows = flat_grad.shape[0] // region_count
    limit = math.sqrt(flat_grad.shape[0] * width)
    sizes = [lax.axis_size(name) for name in REGION_AXES]
    staged = flat_grad.reshape(sizes[0], sizes[1] * sizes[2], share_rows, width)
    staged = exchange_sum(staged, REGION_AXES[1:], 1)
    share = exchange_sum(staged, REGION_AXES[0], 0)
    scene_count = lax.axis_size("scene")
    total_squares = spread_sum(jnp.broadcast_to(jnp.sum(share * share), (8, width)), REGION_AXES)[0, 0]
    factor = jnp.minimum(1.0, limit / jnp.sqrt(total_squares))
    update = spread_sum(share * factor, ("scene",)) / scene_count
    return (block_output.reshape(features.shape), input_grad.reshape(cotangent.shape), update)


def solution(mesh):
    split = jax.sharding.Mesh(
        mesh.devices.reshape(mesh.shape["scene"], 8, 4, 2), ("scene",) + REGION_AXES
    )
    in_specs = (
        P("scene", REGION_AXES, None, None),
        P("scene", REGION_AXES, None),
        P("scene", REGION_AXES, None, None),
        P(),
        P(),
        P("scene", None),
    )
    out_specs = (
        P("scene", REGION_AXES, None, None),
        P("scene", REGION_AXES, None, None),
        P(REGION_AXES, None),
    )
    return jax.shard_map(body, mesh=split, in_specs=in_specs, out_specs=out_specs, check_vma=False)
```

```python
import math

import jax
import jax.numpy as jnp
import numpy as np
from jax import lax
from jax.sharding import PartitionSpec as P

BS = 12
TAPS = 27
GY = 4
GZ = 2


NORM_EPSILON = 1e-06
OFFSETS = [(a, b, c) for a in (-1, 0, 1) for b in (-1, 0, 1) for c in (-1, 0, 1)]
DIRECTIONS = [
    item
    for level in (1, 2, 3)
    for item in OFFSETS
    if abs(item[0]) + abs(item[1]) + abs(item[2]) == level
]
COLUMNS = [(a, b) for a in (-1, 0, 1) for b in (-1, 0, 1)]


def side_range(component, edge):
    if component == 1:
        return (edge - 1, edge)
    if component == -1:
        return (0, 1)
    return (0, edge)


def halo_range(component, edge):
    if component == 1:
        return (edge + 1, edge + 2)
    if component == -1:
        return (0, 1)
    return (1, edge + 1)


def slab_count(direction, edge):
    total = 1
    for component in direction:
        total = total * (1 if component != 0 else edge)
    return total


def row_directions(edge, region_count):
    labels = []
    for position, direction in enumerate(DIRECTIONS):
        labels = labels + [position] * slab_count(direction, edge)
    per_peer = -(-len(labels) // region_count)
    labels = labels + [len(DIRECTIONS)] * (per_peer * region_count - len(labels))
    return (np.array(labels, dtype=np.int32).reshape(per_peer, region_count), len(labels), per_peer)


def plan_sources(owner_row, labels_now, region_count):
    slot_ids = jnp.arange(region_count, dtype=jnp.int32)
    block_of = jnp.sum(
        jnp.where(owner_row[None, :] == slot_ids[:, None], slot_ids[None, :], 0), axis=1
    )
    layer = GY * GZ
    across = region_count // layer
    table = np.array(DIRECTIONS + [(0, 0, 0)], dtype=np.int32)
    real = np.arange(len(DIRECTIONS) + 1) < len(DIRECTIONS)
    pick = labels_now[:, None] == np.arange(len(DIRECTIONS) + 1, dtype=np.int32)[None, :]
    step = jnp.sum(jnp.where(pick[:, :, None], table[None, :, :], 0), axis=1)
    usable = jnp.any(pick & real[None, :], axis=1)
    near_x = (block_of // layer)[:, None] + step[None, :, 0]
    near_y = (block_of // GZ % GY)[:, None] + step[None, :, 1]
    near_z = (block_of % GZ)[:, None] + step[None, :, 2]
    inside = (
        usable[None, :]
        & (near_x >= 0)
        & (near_x < across)
        & (near_y >= 0)
        & (near_y < GY)
        & (near_z >= 0)
        & (near_z < GZ)
    )
    target = near_x * layer + near_y * GZ + near_z
    holder = jnp.sum(
        jnp.where(target[:, :, None] == slot_ids[None, None, :], owner_row[None, None, :], 0), axis=2
    )
    return jnp.where(inside, holder, -1)


def route_plan(owner_row, region_count):
    labels, padded_rows, per_peer = row_directions(BS, region_count)
    myself = lax.axis_index(REGION_AXES)
    labels_now = lax.dynamic_index_in_dim(jnp.asarray(labels), myself, 1, keepdims=False)
    sources = plan_sources(owner_row, labels_now, region_count)
    valid = sources >= 0
    positions = jnp.arange(per_peer, dtype=jnp.int32)[None, :]
    source_rows = jnp.where(valid, sources * per_peer + positions, 0).reshape(-1)
    return (source_rows, valid.astype(jnp.bfloat16), per_peer)


def pick_rows(holdings, plan):
    source_rows, valid, per_peer = plan
    width = holdings.shape[2]
    flat = holdings.reshape(-1, width)
    picked = jnp.take(flat, source_rows, axis=0).reshape(holdings.shape[0], per_peer, width)
    return picked * valid[..., None]


def shell_index(edge, region_count, per_peer):
    cube_ids = np.arange(edge * edge * edge).reshape(edge, edge, edge)
    pieces = []
    for direction in DIRECTIONS:
        spans = [side_range(-component, edge) for component in direction]
        pieces.append(
            cube_ids[
                spans[0][0] : spans[0][1], spans[1][0] : spans[1][1], spans[2][0] : spans[2][1]
            ].reshape(-1)
        )
    rows = np.concatenate(pieces)
    rows = np.pad(rows, (0, per_peer * region_count - rows.size))
    return rows.reshape(per_peer, region_count).T.reshape(-1).astype(np.int32)


def assemble_index(edge, region_count, per_peer):
    side = edge + 2
    inner = edge * edge * edge
    table = np.zeros((side, side, side), np.int64)
    table[1 : edge + 1, 1 : edge + 1, 1 : edge + 1] = np.arange(inner).reshape(edge, edge, edge)
    offset = 0
    for direction in DIRECTIONS:
        spans = [halo_range(component, edge) for component in direction]
        lengths = [upper - lower for lower, upper in spans]
        count = lengths[0] * lengths[1] * lengths[2]
        whole_rows = offset + np.arange(count)
        sources = inner + (whole_rows % region_count) * per_peer + whole_rows // region_count
        table[
            spans[0][0] : spans[0][1], spans[1][0] : spans[1][1], spans[2][0] : spans[2][1]
        ] = sources.reshape(lengths)
        offset = offset + count
    return table.reshape(-1).astype(np.int32)


def dealt_rows(cube, region_count, per_peer):
    width = cube.shape[3]
    index = shell_index(cube.shape[0], region_count, per_peer)
    picked = jnp.take(cube.reshape(-1, width), index, axis=0, mode="clip")
    return picked.reshape(region_count, per_peer, width)


def assemble_rows(received, cube):
    width = cube.shape[3]
    index = assemble_index(cube.shape[0], received.shape[0], received.shape[1])
    source = jnp.concatenate([cube.reshape(-1, width), received.reshape(-1, width)], axis=0)
    return jnp.take(source, index, axis=0, mode="clip")


def relay(plan, cube, region_count):
    dealt = lax.all_to_all(
        dealt_rows(cube, region_count, plan[2]), REGION_AXES, split_axis=0, concat_axis=0, tiled=True
    )
    return lax.all_to_all(pick_rows(dealt, plan), REGION_AXES, split_axis=0, concat_axis=0, tiled=True)


REGION_AXES = ("z", "y", "core")


def direct_scatter_sum(blocks, name, axis):
    size = lax.axis_size(name)
    me = lax.axis_index(name)
    total = lax.dynamic_index_in_dim(blocks, me, axis, keepdims=False)
    for shift in range(1, size):
        piece = lax.dynamic_index_in_dim(blocks, (me + shift) % size, axis, keepdims=False)
        pairs = [(index, (index + shift) % size) for index in range(size)]
        total = total + lax.ppermute(piece, name, pairs)
    return total


def direct_sum(value, names):
    for name in names:
        size = lax.axis_size(name)
        received = [
            lax.ppermute(value, name, [(index, (index + shift) % size) for index in range(size)])
            for shift in range(1, size)
        ]
        for piece in received:
            value = value + piece
    return value


def exchange_sum(blocks, name, axis):
    received = lax.all_to_all(blocks, name, split_axis=axis, concat_axis=axis, tiled=True)
    pieces = [lax.index_in_dim(received, index, axis, keepdims=False) for index in range(blocks.shape[axis])]
    total = pieces[0]
    for piece in pieces[1:]:
        total = total + piece
    return total


def spread_sum(value, names):
    count = math.prod(lax.axis_size(name) for name in names)
    copies = jnp.broadcast_to(value[None], (count,) + value.shape)
    received = lax.all_to_all(copies, names, split_axis=0, concat_axis=0, tiled=True)
    total = received[0]
    for index in range(1, count):
        total = total + received[index]
    return total


def butterfly_sum(value, names):
    for name in names:
        size = lax.axis_size(name)
        stride = 1
        while stride < size:
            pairs = [(index, index ^ stride) for index in range(size)]
            value = value + lax.ppermute(value, name, pairs)
            stride = stride * 2
    return value


def convolve_flat(flat, edge, grad_block, conv_weight):
    side = edge + 2
    width = grad_block.shape[1]
    plane = side * side
    base = plane + side + 1
    span = (edge - 1) * plane + (edge - 1) * side + edge
    zero_row = jnp.zeros((1, 2 * width), flat.dtype)
    after = jnp.concatenate([flat[1:], zero_row], axis=0)
    before = jnp.concatenate([zero_row, flat[:-1]], axis=0)
    act_rows = jnp.concatenate([before[:, :width], flat[:, :width], after[:, :width]], axis=1)
    grad_rows = jnp.concatenate([after[:, width:], flat[:, width:], before[:, width:]], axis=1)
    own = jnp.pad(grad_block.reshape(edge, edge, edge, width), ((1, 1), (1, 1), (1, 1), (0, 0)))
    own = own.reshape(-1, width)[base : base + span]
    forward = jnp.zeros((span, width), jnp.float32)
    backward = jnp.zeros((span, width), jnp.float32)
    terms = []
    for group_index, (shift_x, shift_y) in enumerate(COLUMNS):
        group_weight = conv_weight[3 * group_index : 3 * group_index + 3]
        start = base + shift_x * plane + shift_y * side
        window = act_rows[start : start + span]
        forward = forward + jnp.dot(
            window, group_weight.reshape(3 * width, width), preferred_element_type=jnp.float32
        )
        mirror_start = base - shift_x * plane - shift_y * side
        mirror = grad_rows[mirror_start : mirror_start + span]
        backward = backward + jnp.dot(
            mirror,
            group_weight.transpose(0, 2, 1).reshape(3 * width, width),
            preferred_element_type=jnp.float32,
        )
        terms.append(
            lax.dot_general(window, own, (((0,), (0,)), ((), ())), preferred_element_type=jnp.float32)
        )

    def interior(rows):
        rows = jnp.pad(rows, ((0, edge * plane - span), (0, 0)))
        return rows.reshape(edge, side, side, width)[:, :edge, :edge].reshape(-1, width)

    return (interior(forward), interior(backward), jnp.concatenate(terms, axis=0).reshape(TAPS, width, width))


def body(features, voxel_mask, cotangent, norm_gain, conv_weight, block_owner):
    width = features.shape[-1]
    region_count = math.prod(lax.axis_size(name) for name in REGION_AXES)
    plan = route_plan(block_owner[0], region_count)
    inputs = features[0, 0].astype(jnp.float32)
    mask_col = voxel_mask[0, 0].astype(jnp.float32)[:, None]
    rinv = lax.rsqrt(jnp.mean(inputs * inputs, axis=-1, keepdims=True) + NORM_EPSILON)
    normed = inputs * rinv
    pre = normed * norm_gain
    activity = (jax.nn.silu(pre) * mask_col).astype(jnp.bfloat16)
    grad_out = cotangent[0, 0] * voxel_mask[0, 0].astype(jnp.bfloat16)[:, None]
    act_cube = activity.reshape(BS, BS, BS, width)
    grad_cube = grad_out.reshape(BS, BS, BS, width)
    both_cube = jnp.concatenate([act_cube, grad_cube], axis=-1)
    flat_both = assemble_rows(relay(plan, both_cube, region_count), both_cube)
    forward, backward, weight_grad = convolve_flat(flat_both, BS, grad_out, conv_weight)
    block_output = (inputs + forward * mask_col).astype(jnp.bfloat16)
    slope = jax.nn.sigmoid(pre)
    dnorm = backward * mask_col * (slope * (1.0 + pre * (1.0 - slope))) * norm_gain
    dinput = rinv * (dnorm - normed * jnp.mean(dnorm * normed, axis=-1, keepdims=True))
    input_grad = (cotangent[0, 0].astype(jnp.float32) + dinput).astype(jnp.bfloat16)
    flat_grad = weight_grad.reshape(-1, width)
    share_rows = flat_grad.shape[0] // region_count
    limit = math.sqrt(flat_grad.shape[0] * width)
    sizes = [lax.axis_size(name) for name in REGION_AXES]
    share = exchange_sum(flat_grad.reshape(region_count, share_rows, width), REGION_AXES, 0)
    scene_count = lax.axis_size("scene")
    total_squares = spread_sum(jnp.broadcast_to(jnp.sum(share * share), (8, width)), REGION_AXES)[0, 0]
    factor = jnp.minimum(1.0, limit / jnp.sqrt(total_squares))
    update = spread_sum(share * factor, ("scene",)) / scene_count
    return (block_output.reshape(features.shape), input_grad.reshape(cotangent.shape), update)


def solution(mesh):
    split = jax.sharding.Mesh(
        mesh.devices.reshape(mesh.shape["scene"], 8, 4, 2), ("scene",) + REGION_AXES
    )
    in_specs = (
        P("scene", REGION_AXES, None, None),
        P("scene", REGION_AXES, None),
        P("scene", REGION_AXES, None, None),
        P(),
        P(),
        P("scene", None),
    )
    out_specs = (
        P("scene", REGION_AXES, None, None),
        P("scene", REGION_AXES, None, None),
        P(REGION_AXES, None),
    )
    return jax.shard_map(body, mesh=split, in_specs=in_specs, out_specs=out_specs, check_vma=False)
```

```python
import math

import jax
import jax.numpy as jnp
import numpy as np
from jax import lax
from jax.sharding import PartitionSpec as P

BS = 12
TAPS = 27
GY = 4
GZ = 2


NORM_EPSILON = 1e-06
OFFSETS = [(a, b, c) for a in (-1, 0, 1) for b in (-1, 0, 1) for c in (-1, 0, 1)]
DIRECTIONS = [
    item
    for level in (1, 2, 3)
    for item in OFFSETS
    if abs(item[0]) + abs(item[1]) + abs(item[2]) == level
]
COLUMNS = [(a, b) for a in (-1, 0, 1) for b in (-1, 0, 1)]


def side_range(component, edge):
    if component == 1:
        return (edge - 1, edge)
    if component == -1:
        return (0, 1)
    return (0, edge)


def halo_range(component, edge):
    if component == 1:
        return (edge + 1, edge + 2)
    if component == -1:
        return (0, 1)
    return (1, edge + 1)


def slab_count(direction, edge):
    total = 1
    for component in direction:
        total = total * (1 if component != 0 else edge)
    return total


def row_directions(edge, region_count):
    labels = []
    for position, direction in enumerate(DIRECTIONS):
        labels = labels + [position] * slab_count(direction, edge)
    per_peer = -(-len(labels) // region_count)
    labels = labels + [len(DIRECTIONS)] * (per_peer * region_count - len(labels))
    return (np.array(labels, dtype=np.int32).reshape(per_peer, region_count), len(labels), per_peer)


def plan_sources(owner_row, labels_now, region_count):
    slot_ids = jnp.arange(region_count, dtype=jnp.int32)
    block_of = jnp.sum(
        jnp.where(owner_row[None, :] == slot_ids[:, None], slot_ids[None, :], 0), axis=1
    )
    layer = GY * GZ
    across = region_count // layer
    table = np.array(DIRECTIONS + [(0, 0, 0)], dtype=np.int32)
    real = np.arange(len(DIRECTIONS) + 1) < len(DIRECTIONS)
    pick = labels_now[:, None] == np.arange(len(DIRECTIONS) + 1, dtype=np.int32)[None, :]
    step = jnp.sum(jnp.where(pick[:, :, None], table[None, :, :], 0), axis=1)
    usable = jnp.any(pick & real[None, :], axis=1)
    near_x = (block_of // layer)[:, None] + step[None, :, 0]
    near_y = (block_of // GZ % GY)[:, None] + step[None, :, 1]
    near_z = (block_of % GZ)[:, None] + step[None, :, 2]
    inside = (
        usable[None, :]
        & (near_x >= 0)
        & (near_x < across)
        & (near_y >= 0)
        & (near_y < GY)
        & (near_z >= 0)
        & (near_z < GZ)
    )
    target = near_x * layer + near_y * GZ + near_z
    holder = jnp.sum(
        jnp.where(target[:, :, None] == slot_ids[None, None, :], owner_row[None, None, :], 0), axis=2
    )
    return jnp.where(inside, holder, -1)


def route_plan(owner_row, region_count):
    labels, padded_rows, per_peer = row_directions(BS, region_count)
    myself = lax.axis_index(REGION_AXES)
    labels_now = lax.dynamic_index_in_dim(jnp.asarray(labels), myself, 1, keepdims=False)
    sources = plan_sources(owner_row, labels_now, region_count)
    valid = sources >= 0
    positions = jnp.arange(per_peer, dtype=jnp.int32)[None, :]
    source_rows = jnp.where(valid, sources * per_peer + positions, 0).reshape(-1)
    return (source_rows, valid.astype(jnp.bfloat16), per_peer)


def pick_rows(holdings, plan):
    source_rows, valid, per_peer = plan
    width = holdings.shape[2]
    flat = holdings.reshape(-1, width)
    picked = jnp.take(flat, source_rows, axis=0).reshape(holdings.shape[0], per_peer, width)
    return picked * valid[..., None]


def shell_index(edge, region_count, per_peer):
    cube_ids = np.arange(edge * edge * edge).reshape(edge, edge, edge)
    pieces = []
    for direction in DIRECTIONS:
        spans = [side_range(-component, edge) for component in direction]
        pieces.append(
            cube_ids[
                spans[0][0] : spans[0][1], spans[1][0] : spans[1][1], spans[2][0] : spans[2][1]
            ].reshape(-1)
        )
    rows = np.concatenate(pieces)
    rows = np.pad(rows, (0, per_peer * region_count - rows.size))
    return rows.reshape(per_peer, region_count).T.reshape(-1).astype(np.int32)


def assemble_index(edge, region_count, per_peer):
    side = edge + 2
    inner = edge * edge * edge
    table = np.zeros((side, side, side), np.int64)
    table[1 : edge + 1, 1 : edge + 1, 1 : edge + 1] = np.arange(inner).reshape(edge, edge, edge)
    offset = 0
    for direction in DIRECTIONS:
        spans = [halo_range(component, edge) for component in direction]
        lengths = [upper - lower for lower, upper in spans]
        count = lengths[0] * lengths[1] * lengths[2]
        whole_rows = offset + np.arange(count)
        sources = inner + (whole_rows % region_count) * per_peer + whole_rows // region_count
        table[
            spans[0][0] : spans[0][1], spans[1][0] : spans[1][1], spans[2][0] : spans[2][1]
        ] = sources.reshape(lengths)
        offset = offset + count
    return table.reshape(-1).astype(np.int32)


def dealt_rows(cube, region_count, per_peer):
    width = cube.shape[3]
    index = shell_index(cube.shape[0], region_count, per_peer)
    picked = jnp.take(cube.reshape(-1, width), index, axis=0, mode="clip")
    return picked.reshape(region_count, per_peer, width)


def assemble_rows(received, cube):
    width = cube.shape[3]
    index = assemble_index(cube.shape[0], received.shape[0], received.shape[1])
    source = jnp.concatenate([cube.reshape(-1, width), received.reshape(-1, width)], axis=0)
    return jnp.take(source, index, axis=0, mode="clip")


def relay(plan, cube, region_count):
    dealt = lax.all_to_all(
        dealt_rows(cube, region_count, plan[2]), REGION_AXES, split_axis=0, concat_axis=0, tiled=True
    )
    return lax.all_to_all(pick_rows(dealt, plan), REGION_AXES, split_axis=0, concat_axis=0, tiled=True)


REGION_AXES = ("z", "y", "core")


def direct_scatter_sum(blocks, name, axis):
    size = lax.axis_size(name)
    me = lax.axis_index(name)
    total = lax.dynamic_index_in_dim(blocks, me, axis, keepdims=False)
    for shift in range(1, size):
        piece = lax.dynamic_index_in_dim(blocks, (me + shift) % size, axis, keepdims=False)
        pairs = [(index, (index + shift) % size) for index in range(size)]
        total = total + lax.ppermute(piece, name, pairs)
    return total


def direct_sum(value, names):
    for name in names:
        size = lax.axis_size(name)
        received = [
            lax.ppermute(value, name, [(index, (index + shift) % size) for index in range(size)])
            for shift in range(1, size)
        ]
        for piece in received:
            value = value + piece
    return value


def exchange_sum(blocks, name, axis):
    received = lax.all_to_all(blocks, name, split_axis=axis, concat_axis=axis, tiled=True)
    pieces = [lax.index_in_dim(received, index, axis, keepdims=False) for index in range(blocks.shape[axis])]
    total = pieces[0]
    for piece in pieces[1:]:
        total = total + piece
    return total


def spread_sum(value, names):
    count = math.prod(lax.axis_size(name) for name in names)
    copies = jnp.broadcast_to(value[None], (count,) + value.shape)
    received = lax.all_to_all(copies, names, split_axis=0, concat_axis=0, tiled=True)
    total = received[0]
    for index in range(1, count):
        total = total + received[index]
    return total


def butterfly_sum(value, names):
    for name in names:
        size = lax.axis_size(name)
        stride = 1
        while stride < size:
            pairs = [(index, index ^ stride) for index in range(size)]
            value = value + lax.ppermute(value, name, pairs)
            stride = stride * 2
    return value


def convolve_flat(flat, edge, grad_block, conv_weight):
    side = edge + 2
    width = grad_block.shape[1]
    plane = side * side
    base = plane + side + 1
    span = (edge - 1) * plane + (edge - 1) * side + edge
    zero_row = jnp.zeros((1, 2 * width), flat.dtype)
    after = jnp.concatenate([flat[1:], zero_row], axis=0)
    before = jnp.concatenate([zero_row, flat[:-1]], axis=0)
    act_rows = jnp.concatenate([before[:, :width], flat[:, :width], after[:, :width]], axis=1)
    grad_rows = jnp.concatenate([after[:, width:], flat[:, width:], before[:, width:]], axis=1)
    own = jnp.pad(grad_block.reshape(edge, edge, edge, width), ((1, 1), (1, 1), (1, 1), (0, 0)))
    own = own.reshape(-1, width)[base : base + span]
    forward = jnp.zeros((span, width), jnp.float32)
    backward = jnp.zeros((span, width), jnp.float32)
    terms = []
    for group_index, (shift_x, shift_y) in enumerate(COLUMNS):
        group_weight = conv_weight[3 * group_index : 3 * group_index + 3]
        start = base + shift_x * plane + shift_y * side
        window = act_rows[start : start + span]
        forward = forward + jnp.dot(
            window, group_weight.reshape(3 * width, width), preferred_element_type=jnp.float32
        )
        mirror_start = base - shift_x * plane - shift_y * side
        mirror = grad_rows[mirror_start : mirror_start + span]
        backward = backward + jnp.dot(
            mirror,
            group_weight.transpose(0, 2, 1).reshape(3 * width, width),
            preferred_element_type=jnp.float32,
        )
        terms.append(
            lax.dot_general(window, own, (((0,), (0,)), ((), ())), preferred_element_type=jnp.float32)
        )

    def interior(rows):
        rows = jnp.pad(rows, ((0, edge * plane - span), (0, 0)))
        return rows.reshape(edge, side, side, width)[:, :edge, :edge].reshape(-1, width)

    return (interior(forward), interior(backward), jnp.concatenate(terms, axis=0).reshape(TAPS, width, width))


def body(features, voxel_mask, cotangent, norm_gain, conv_weight, block_owner):
    width = features.shape[-1]
    region_count = math.prod(lax.axis_size(name) for name in REGION_AXES)
    plan = route_plan(block_owner[0], region_count)
    inputs = features[0, 0].astype(jnp.float32)
    mask_col = voxel_mask[0, 0].astype(jnp.float32)[:, None]
    rinv = lax.rsqrt(jnp.mean(inputs * inputs, axis=-1, keepdims=True) + NORM_EPSILON)
    normed = inputs * rinv
    pre = normed * norm_gain
    activity = (jax.nn.silu(pre) * mask_col).astype(jnp.bfloat16)
    grad_out = cotangent[0, 0] * voxel_mask[0, 0].astype(jnp.bfloat16)[:, None]
    act_cube = activity.reshape(BS, BS, BS, width)
    grad_cube = grad_out.reshape(BS, BS, BS, width)
    both_cube = jnp.concatenate([act_cube, grad_cube], axis=-1)
    flat_both = assemble_rows(relay(plan, both_cube, region_count), both_cube)
    forward, backward, weight_grad = convolve_flat(flat_both, BS, grad_out, conv_weight)
    block_output = (inputs + forward * mask_col).astype(jnp.bfloat16)
    slope = jax.nn.sigmoid(pre)
    dnorm = backward * mask_col * (slope * (1.0 + pre * (1.0 - slope))) * norm_gain
    dinput = rinv * (dnorm - normed * jnp.mean(dnorm * normed, axis=-1, keepdims=True))
    input_grad = (cotangent[0, 0].astype(jnp.float32) + dinput).astype(jnp.bfloat16)
    flat_grad = weight_grad.reshape(-1, width)
    share_rows = flat_grad.shape[0] // region_count
    limit = math.sqrt(flat_grad.shape[0] * width)
    sizes = [lax.axis_size(name) for name in REGION_AXES]
    staged = flat_grad.reshape(sizes[0], sizes[1] * sizes[2], share_rows, width)
    staged = exchange_sum(staged, REGION_AXES[1:], 1)
    share = exchange_sum(staged, REGION_AXES[0], 0)
    scene_count = lax.axis_size("scene")
    total_squares = spread_sum(jnp.broadcast_to(jnp.sum(share * share), (1, width)), REGION_AXES)[0, 0]
    factor = jnp.minimum(1.0, limit / jnp.sqrt(total_squares))
    update = spread_sum(share * factor, ("scene",)) / scene_count
    return (block_output.reshape(features.shape), input_grad.reshape(cotangent.shape), update)


def solution(mesh):
    split = jax.sharding.Mesh(
        mesh.devices.reshape(mesh.shape["scene"], 8, 4, 2), ("scene",) + REGION_AXES
    )
    in_specs = (
        P("scene", REGION_AXES, None, None),
        P("scene", REGION_AXES, None),
        P("scene", REGION_AXES, None, None),
        P(),
        P(),
        P("scene", None),
    )
    out_specs = (
        P("scene", REGION_AXES, None, None),
        P("scene", REGION_AXES, None, None),
        P(REGION_AXES, None),
    )
    return jax.shard_map(body, mesh=split, in_specs=in_specs, out_specs=out_specs, check_vma=False)
```
